512 devices in a mesh: lon: 32 (over z_lo, x, core), lat: 16 (over y, z_hi).
Axes of the slice: x: 4, y: 4, z: 16 (z_hi: 4, z_lo: 4; z = z_hi * 4 + z_lo), core: 2. Of those that a mesh axis runs over, the one named last changes fastest.
Arguments:
- ensemble: float32 [9, 40, 128, 4096], P(None, None, 'lat', 'lon'), may hold values from -6 to 6
- obs_lon: int32 [512], replicated, may hold values from 0 to 4095
- obs_lat: int32 [512], replicated, may hold values from 0 to 127
- observation_field: int32 [512], replicated, may hold values from 0 to 8
- obs_radius: int32 [512], replicated, may hold values from 4 to 8
- batch_order: int32 [512], replicated, may hold values from 0 to 511, each once
- obs_value: float32 [512], replicated, may hold values from -8 to 8
- obs_error: float32 [512], replicated, may hold values from 0.1 to 1
Outputs:
- analysis: bfloat16 [9, 40, 128, 4096], P(None, None, 'lat', 'lon')
The draws below stay inside these ranges and needn't reach their ends.
Inputs may be any that keep to these rules, and one draw needn't show every extreme that they name: `batch_order`: every observation number appears once. `obs_radius`: radii are at most 8 cells.
All inputs are finite; a program needn't handle non-finite values.
Results may differ from the reference program's by a relative error of at most 0.001.
Values sent between devices are 32-bit elements; how exact they have to be, the bound alone decides.
No kernel may reach another device: no remote copies, remote signals or barrier semaphores. Data moves between devices by JAX's collectives and lax.ppermute only.
A program may use at most 64 MiB of HBM per device.

```python
import math
import jax
import jax.numpy as jnp
import numpy as np
from jax import lax

CY = 8
MEMBERS = 40
STATE_FIELDS = 9
STEPS = 2
BATCHES = 2
NB = 256
NOBS = 512
NX = 4096
NY = 128


def touch_ends(result, stream_key, low, top_value):
    spot = [jax.random.randint(jax.random.fold_in(stream_key, axis), (), 0, length) for axis, length in enumerate(result.shape)]
    widest = result.shape.index(max(result.shape))
    neighbour = spot[:widest] + [(spot[widest] + 1) % result.shape[widest]] + spot[widest + 1:]
    return result.at[tuple(spot)].set(low).at[tuple(neighbour)].set(top_value)


def level_of(stream_key, dims, shards, least, largest):
    level = 1.0
    for axis_at, shards_of in shards:
        draws = jax.random.uniform(jax.random.fold_in(jax.random.fold_in(stream_key, 6), axis_at), (shards_of,), jnp.float32, least / len(shards), largest / len(shards))
        level = level * jnp.repeat(jnp.exp(draws), dims[axis_at] // shards_of).reshape((-1,) + (1,) * (len(dims) - 1 - axis_at))
    return level


def rank_bounds(count, lean):
    loads = [(1 << 20) // math.isqrt(rank ** lean) + 1 for rank in range(1, count + 1)]
    spread = 1 + sum(loads) // (1 << 30)
    return np.cumsum(np.array([max(1, weight // spread) for weight in loads]))


def ranked(rng, dims, count, lean):
    table = rank_bounds(count, lean)
    lot = jax.random.randint(jax.random.fold_in(rng, 1), dims, 0, int(table[count - 1]))
    standing = jnp.searchsorted(jnp.asarray(table, jnp.int32), lot, side="right")
    return jax.random.permutation(jax.random.fold_in(rng, 2), count)[standing].astype(jnp.int32)


def noise(own_key, shape, spread, bound, cuts=(), kind=jnp.bfloat16):
    loudness = level_of(own_key, shape, cuts, -0.22, 0.18) if cuts else 1.0
    values = jax.random.normal(own_key, shape, jnp.float32) * spread * loudness
    return jnp.minimum(jnp.maximum(values, -bound), bound).astype(kind)


def setup_inputs(seed: int = 0) -> dict:
    streams_of = jax.random.split(jax.random.key(seed), 9)
    ensemble = noise(streams_of[0], (STATE_FIELDS, MEMBERS, NY, NX), 1.0, 6.0, ((2, 16), (3, 32)), jnp.float32)
    obs_lon = touch_ends(jax.random.randint(streams_of[1], (NOBS,), 0, NX), jax.random.fold_in(streams_of[1], 1), 0, NX - 1).astype(jnp.int32)
    obs_lat = touch_ends(ranked(streams_of[2], (NOBS,), NY, 2), jax.random.fold_in(streams_of[2], 3), 0, NY - 1).astype(jnp.int32)
    observation_field = touch_ends(jax.random.randint(streams_of[3], (NOBS,), 0, STATE_FIELDS), jax.random.fold_in(streams_of[3], 1), 0, STATE_FIELDS - 1).astype(jnp.int32)
    obs_radius = touch_ends(jax.random.randint(streams_of[4], (NOBS,), CY // 2, CY + 1), jax.random.fold_in(streams_of[4], 1), CY // 2, CY).astype(jnp.int32)
    batch_order = jax.random.permutation(streams_of[5], NOBS).astype(jnp.int32)
    obs_value = noise(streams_of[6], (NOBS,), 2.0, 8.0, (), jnp.float32)
    obs_error = jnp.clip(jnp.exp(jax.random.uniform(streams_of[7], (NOBS,), jnp.float32, math.log(0.1), math.log(1.0))), 0.1, 1.0)
    return {"ensemble": ensemble, "obs_lon": obs_lon, "obs_lat": obs_lat, "observation_field": observation_field, "obs_radius": obs_radius, "batch_order": batch_order, "obs_value": obs_value, "obs_error": obs_error}


RATE = 0.4
DEPTHS = (1.0, 0.6, 0.35)
COUPLE = ((1.0, 0.5, 0.25), (0.5, 1.0, 0.5), (0.25, 0.5, 1.0))

def couple(height):
    return jnp.stack([COUPLE[k][0] * height[0] + COUPLE[k][1] * height[1] + COUPLE[k][2] * height[2] for k in range(3)])

def zonal(values):
    return 0.5 * (jnp.roll(values, -1, axis=3) - jnp.roll(values, 1, axis=3))

def meridional(values):
    padded = jnp.pad(values, ((0, 0), (0, 0), (1, 1), (0, 0)))
    return 0.5 * (padded[:, :, 2:, :] - padded[:, :, :-2, :])

def march_prediction(running_member_set, rotation_frequency):
    height = running_member_set[0:3]
    eastward_speed = running_member_set[3:6]
    merid_vel = running_member_set[6:9]
    depths = jnp.array(DEPTHS, jnp.float32)[:, None, None, None]
    height = height - RATE * depths * (zonal(eastward_speed) + meridional(merid_vel))
    pressure = couple(height)
    eastward_speed = eastward_speed + RATE * rotation_frequency * merid_vel - RATE * zonal(pressure)
    merid_vel = merid_vel - RATE * rotation_frequency * eastward_speed - RATE * meridional(pressure)
    return jnp.concatenate([height, eastward_speed, merid_vel])

def statistics(priors, values, errors, member_count):
    mean_obs = lax.optimization_barrier(jnp.mean(priors, axis=1, keepdims=True))
    anomaly = priors - mean_obs
    variance = lax.optimization_barrier(jnp.sum(anomaly * anomaly, axis=1, keepdims=True)) / (member_count - 1)
    obs_err = errors[:, None]
    denominator = variance + obs_err
    shrink = 1.0 / (1.0 + jnp.sqrt(obs_err / denominator))
    gains = (values[:, None] - mean_obs - shrink * anomaly) / denominator
    return (gains, anomaly)

def localize(cell_lon, cell_lat, lon_obs, lat_obs, radius_obs, grid_lon):
    lon_gap = (cell_lon[None, :] - lon_obs[:, None]) % grid_lon
    lon_gap = jnp.minimum(lon_gap, grid_lon - lon_gap)
    lat_gap = cell_lat[None, :] - lat_obs[:, None]
    distance_sq = (lon_gap * lon_gap + lat_gap * lat_gap).astype(jnp.float32)
    radius_sq = (radius_obs * radius_obs).astype(jnp.float32)[:, None]
    return jnp.square(jnp.maximum(1.0 - distance_sq / radius_sq, 0.0))

def reference(ensemble, obs_lon, obs_lat, observation_field, obs_radius, batch_order, obs_value, obs_error):
    rows_all = jnp.arange(NY, dtype=jnp.float32)
    rotation_frequency = (2.0 * jnp.sin(math.pi * ((rows_all + 0.5) / NY - 0.5)))[:, None]
    running_member_set = ensemble
    for step_index in range(STEPS):
        running_member_set = march_prediction(running_member_set, rotation_frequency)
    columns = jnp.arange(NX, dtype=jnp.int32)
    for batch_index in range(BATCHES):
        batch_ids = batch_order[batch_index * NB:(batch_index + 1) * NB]
        lon_obs = obs_lon[batch_ids]
        lat_obs = obs_lat[batch_ids]
        kind_obs = observation_field[batch_ids]
        radius_obs = obs_radius[batch_ids]
        priors = running_member_set[kind_obs, :, lat_obs, lon_obs]
        gains, anomaly = statistics(priors, obs_value[batch_ids], obs_error[batch_ids], MEMBERS)

        def update_row(row_index, current):
            row_index = jnp.asarray(row_index).astype(jnp.int32)
            row_block = lax.dynamic_slice_in_dim(current, row_index, 1, 2)[:, :, 0, :]
            cell_lat = jnp.zeros((NX,), jnp.int32) + row_index
            weights = localize(columns, cell_lat, lon_obs, lat_obs, radius_obs, NX)
            deviation = row_block - lax.optimization_barrier(jnp.mean(row_block, axis=1, keepdims=True))
            covariance = jnp.einsum('om,fmc->foc', anomaly, deviation, precision=lax.Precision.HIGHEST) / (MEMBERS - 1)
            increment = jnp.einsum('om,foc->fmc', gains, covariance * weights[None], precision=lax.Precision.HIGHEST)
            return lax.dynamic_update_slice_in_dim(current, (row_block + increment)[:, :, None, :], row_index, 2)
        running_member_set = lax.fori_loop(0, NY, update_row, running_member_set)
    return running_member_set.astype(jnp.bfloat16)
```

```python
import math

import jax
import jax.numpy as jnp
from jax import lax
from jax.sharding import PartitionSpec as P

STEPS = 2
BATCHES = 2
NB = 256


RATE = 0.4
DEPTHS = (1.0, 0.6, 0.35)
COUPLE = ((1.0, 0.5, 0.25), (0.5, 1.0, 0.5), (0.25, 0.5, 1.0))


def lon_edges(array):
    size = lax.axis_size("lon")
    up = [(i, (i + 1) % size) for i in range(size)]
    down = [((i + 1) % size, i) for i in range(size)]
    left = lax.ppermute(array[..., -1:], "lon", up)
    right = lax.ppermute(array[..., :1], "lon", down)
    return left, right


def lat_edges(array):
    size = lax.axis_size("lat")
    up = [(i, i + 1) for i in range(size - 1)]
    down = [(i + 1, i) for i in range(size - 1)]
    before = lax.ppermute(array[:, :, -1:, :], "lat", up)
    after = lax.ppermute(array[:, :, :1, :], "lat", down)
    return before, after


def zonal(values, left, right):
    following = jnp.concatenate([values[..., 1:], right], axis=3)
    preceding = jnp.concatenate([left, values[..., :-1]], axis=3)
    return 0.5 * (following - preceding)


def meridional(values, before, after):
    following = jnp.concatenate([values[:, :, 1:, :], after], axis=2)
    preceding = jnp.concatenate([before, values[:, :, :-1, :]], axis=2)
    return 0.5 * (following - preceding)


def couple(height):
    return jnp.stack(
        [
            COUPLE[k][0] * height[0] + COUPLE[k][1] * height[1] + COUPLE[k][2] * height[2]
            for k in range(3)
        ]
    )


def march_prediction(running_member_set, rotation_frequency):
    height = running_member_set[0:3]
    eastward_speed = running_member_set[3:6]
    merid_vel = running_member_set[6:9]
    depths = jnp.array(DEPTHS, jnp.float32)[:, None, None, None]
    u_left, u_right = lon_edges(eastward_speed)
    v_before, v_after = lat_edges(merid_vel)
    height = height - RATE * depths * (
        zonal(eastward_speed, u_left, u_right) + meridional(merid_vel, v_before, v_after)
    )
    pressure = couple(height)
    p_left, p_right = lon_edges(pressure)
    p_before, p_after = lat_edges(pressure)
    eastward_speed = (
        eastward_speed
        + RATE * rotation_frequency * merid_vel
        - RATE * zonal(pressure, p_left, p_right)
    )
    merid_vel = (
        merid_vel
        - RATE * rotation_frequency * eastward_speed
        - RATE * meridional(pressure, p_before, p_after)
    )
    return jnp.concatenate([height, eastward_speed, merid_vel])


def statistics(priors, values, errors, member_count):
    mean_obs = jnp.mean(priors, axis=1, keepdims=True)
    anomaly = priors - mean_obs
    variance = jnp.sum(anomaly * anomaly, axis=1, keepdims=True) / (member_count - 1)
    obs_err = errors[:, None]
    denominator = variance + obs_err
    shrink = 1.0 / (1.0 + jnp.sqrt(obs_err / denominator))
    gains = (values[:, None] - mean_obs - shrink * anomaly) / denominator
    return (gains, anomaly)


def localize(cell_lon, cell_lat, lon_obs, lat_obs, radius_obs, grid_lon):
    lon_gap = (cell_lon[None, :] - lon_obs[:, None]) % grid_lon
    lon_gap = jnp.minimum(lon_gap, grid_lon - lon_gap)
    lat_gap = cell_lat[None, :] - lat_obs[:, None]
    distance_sq = (lon_gap * lon_gap + lat_gap * lat_gap).astype(jnp.float32)
    radius_sq = (radius_obs * radius_obs).astype(jnp.float32)[:, None]
    return jnp.square(jnp.maximum(1.0 - distance_sq / radius_sq, 0.0))


def neighbourhood_sum(table):
    lon_n = lax.axis_size("lon")
    lat_n = lax.axis_size("lat")
    total = table
    for dlon in (-1, 0, 1):
        for dlat in (-1, 0, 1):
            if dlon == 0 and dlat == 0:
                continue
            pairs = []
            for i in range(lon_n):
                for j in range(lat_n):
                    jj = j + dlat
                    if 0 <= jj < lat_n:
                        pairs.append((i * lat_n + j, ((i + dlon) % lon_n) * lat_n + jj))
            total = total + lax.ppermute(table, ("lon", "lat"), pairs)
    return total


def assimilate(
    running_member_set,
    batch_ids,
    obs_lon,
    obs_lat,
    observation_field,
    obs_radius,
    obs_value,
    obs_error,
):
    fields_count, member_count, rows_tile, cols_tile = running_member_set.shape
    lon_base = lax.axis_index("lon") * cols_tile
    lat_base = lax.axis_index("lat") * rows_tile
    grid_lon = cols_tile * lax.axis_size("lon")
    lon_obs = obs_lon[batch_ids]
    lat_obs = obs_lat[batch_ids]
    kind_obs = observation_field[batch_ids]
    owned = (
        (lon_obs >= lon_base)
        & (lon_obs < lon_base + cols_tile)
        & (lat_obs >= lat_base)
        & (lat_obs < lat_base + rows_tile)
    )
    nearby_latitude = jnp.clip(lat_obs - lat_base, 0, rows_tile - 1)
    local_lon = jnp.clip(lon_obs - lon_base, 0, cols_tile - 1)
    at_owner = running_member_set[kind_obs, :, nearby_latitude, local_lon]
    at_owner = jnp.where(owned[:, None], at_owner, 0.0)
    priors = neighbourhood_sum(at_owner)
    gains, anomaly = statistics(priors, obs_value[batch_ids], obs_error[batch_ids], member_count)
    cell_lat = lat_base + jnp.repeat(jnp.arange(rows_tile, dtype=jnp.int32), cols_tile)
    cell_lon = lon_base + jnp.tile(jnp.arange(cols_tile, dtype=jnp.int32), rows_tile)
    weights = localize(cell_lon, cell_lat, lon_obs, lat_obs, obs_radius[batch_ids], grid_lon)
    flattened = running_member_set.reshape(fields_count, member_count, rows_tile * cols_tile)
    deviation = flattened - jnp.mean(flattened, axis=1, keepdims=True)
    covariance = jnp.einsum(
        "om,fmc->foc", anomaly, deviation, precision=lax.Precision.HIGHEST
    ) / (member_count - 1)
    increment = jnp.einsum(
        "om,foc->fmc", gains, covariance * weights[None], precision=lax.Precision.HIGHEST
    )
    return (flattened + increment).reshape(running_member_set.shape)


def shards(
    ensemble, obs_lon, obs_lat, observation_field, obs_radius, batch_order, obs_value, obs_error
):
    rows_tile = ensemble.shape[2]
    lat_index = lax.axis_index("lat")
    lat_count = lax.axis_size("lat")
    mesh_northing = rows_tile * lat_count
    row_global = (lat_index * rows_tile + jnp.arange(rows_tile, dtype=jnp.int32)).astype(
        jnp.float32
    )
    rotation_frequency = (2.0 * jnp.sin(math.pi * ((row_global + 0.5) / mesh_northing - 0.5)))[
        :, None
    ]
    running_member_set = ensemble
    for step_index in range(STEPS):
        running_member_set = march_prediction(running_member_set, rotation_frequency)
    for batch_index in range(BATCHES):
        batch_ids = batch_order[batch_index * NB : (batch_index + 1) * NB]
        running_member_set = assimilate(
            running_member_set,
            batch_ids,
            obs_lon,
            obs_lat,
            observation_field,
            obs_radius,
            obs_value,
            obs_error,
        )
    return running_member_set.astype(jnp.bfloat16)


def solution(mesh):
    placed = (P(None, None, "lat", "lon"), P(), P(), P(), P(), P(), P(), P())
    return jax.shard_map(
        shards, mesh=mesh, in_specs=placed, out_specs=P(None, None, "lat", "lon"), check_vma=False
    )
```

```python
import math

import jax
import jax.numpy as jnp
from jax import lax
from jax.sharding import PartitionSpec as P

STEPS = 2
BATCHES = 2
NB = 256


RATE = 0.4
DEPTHS = (1.0, 0.6, 0.35)
COUPLE = ((1.0, 0.5, 0.25), (0.5, 1.0, 0.5), (0.25, 0.5, 1.0))


def lon_edges(array):
    size = lax.axis_size("lon")
    up = [(i, (i + 1) % size) for i in range(size)]
    down = [((i + 1) % size, i) for i in range(size)]
    left = lax.ppermute(array[..., -1:], "lon", up)
    right = lax.ppermute(array[..., :1], "lon", down)
    return left, right


def lat_edges(array):
    size = lax.axis_size("lat")
    up = [(i, i + 1) for i in range(size - 1)]
    down = [(i + 1, i) for i in range(size - 1)]
    before = lax.ppermute(array[:, :, -1:, :], "lat", up)
    after = lax.ppermute(array[:, :, :1, :], "lat", down)
    return before, after


def zonal(values, left, right):
    following = jnp.concatenate([values[..., 1:], right], axis=3)
    preceding = jnp.concatenate([left, values[..., :-1]], axis=3)
    return 0.5 * (following - preceding)


def meridional(values, before, after):
    following = jnp.concatenate([values[:, :, 1:, :], after], axis=2)
    preceding = jnp.concatenate([before, values[:, :, :-1, :]], axis=2)
    return 0.5 * (following - preceding)


def couple(height):
    return jnp.stack(
        [
            COUPLE[k][0] * height[0] + COUPLE[k][1] * height[1] + COUPLE[k][2] * height[2]
            for k in range(3)
        ]
    )


def march_prediction(running_member_set, rotation_frequency):
    height = running_member_set[0:3]
    eastward_speed = running_member_set[3:6]
    merid_vel = running_member_set[6:9]
    depths = jnp.array(DEPTHS, jnp.float32)[:, None, None, None]
    u_left, u_right = lon_edges(eastward_speed)
    v_before, v_after = lat_edges(merid_vel)
    height = height - RATE * depths * (
        zonal(eastward_speed, u_left, u_right) + meridional(merid_vel, v_before, v_after)
    )
    pressure = couple(height)
    p_left, p_right = lon_edges(pressure)
    p_before, p_after = lat_edges(pressure)
    eastward_speed = (
        eastward_speed
        + RATE * rotation_frequency * merid_vel
        - RATE * zonal(pressure, p_left, p_right)
    )
    merid_vel = (
        merid_vel
        - RATE * rotation_frequency * eastward_speed
        - RATE * meridional(pressure, p_before, p_after)
    )
    return jnp.concatenate([height, eastward_speed, merid_vel])


def statistics(priors, values, errors, member_count):
    mean_obs = jnp.mean(priors, axis=1, keepdims=True)
    anomaly = priors - mean_obs
    variance = jnp.sum(anomaly * anomaly, axis=1, keepdims=True) / (member_count - 1)
    obs_err = errors[:, None]
    denominator = variance + obs_err
    shrink = 1.0 / (1.0 + jnp.sqrt(obs_err / denominator))
    gains = (values[:, None] - mean_obs - shrink * anomaly) / denominator
    return (gains, anomaly)


def localize(cell_lon, cell_lat, lon_obs, lat_obs, radius_obs, grid_lon):
    lon_gap = (cell_lon[None, :] - lon_obs[:, None]) % grid_lon
    lon_gap = jnp.minimum(lon_gap, grid_lon - lon_gap)
    lat_gap = cell_lat[None, :] - lat_obs[:, None]
    distance_sq = (lon_gap * lon_gap + lat_gap * lat_gap).astype(jnp.float32)
    radius_sq = (radius_obs * radius_obs).astype(jnp.float32)[:, None]
    return jnp.square(jnp.maximum(1.0 - distance_sq / radius_sq, 0.0))


def tile_origin(state):
    _, _, rows_tile, cols_tile = state.shape
    return lax.axis_index("lon") * cols_tile, lax.axis_index("lat") * rows_tile


def at_owner(state, lon_obs, lat_obs, kind_obs):
    _, _, rows_tile, cols_tile = state.shape
    lon_base, lat_base = tile_origin(state)
    owned = (
        (lon_obs >= lon_base)
        & (lon_obs < lon_base + cols_tile)
        & (lat_obs >= lat_base)
        & (lat_obs < lat_base + rows_tile)
    )
    nearby_latitude = jnp.clip(lat_obs - lat_base, 0, rows_tile - 1)
    local_lon = jnp.clip(lon_obs - lon_base, 0, cols_tile - 1)
    values = state[kind_obs, :, nearby_latitude, local_lon]
    return values, owned


def update(state, gains, anomaly, weights):
    fields_count, member_count, rows_tile, cols_tile = state.shape
    flattened = state.reshape(fields_count, member_count, rows_tile * cols_tile)
    deviation = flattened - jnp.mean(flattened, axis=1, keepdims=True)
    covariance = jnp.einsum(
        "om,fmc->foc", anomaly, deviation, precision=lax.Precision.HIGHEST
    ) / (member_count - 1)
    increment = jnp.einsum(
        "om,foc->fmc", gains, covariance * weights[None], precision=lax.Precision.HIGHEST
    )
    return (flattened + increment).reshape(state.shape)


def tile_weights(state, lon_obs, lat_obs, radius_obs):
    _, _, rows_tile, cols_tile = state.shape
    lon_base, lat_base = tile_origin(state)
    grid_lon = cols_tile * lax.axis_size("lon")
    cell_lat = lat_base + jnp.repeat(jnp.arange(rows_tile, dtype=jnp.int32), cols_tile)
    cell_lon = lon_base + jnp.tile(jnp.arange(cols_tile, dtype=jnp.int32), rows_tile)
    return localize(cell_lon, cell_lat, lon_obs, lat_obs, radius_obs, grid_lon)


def shards(
    ensemble, obs_lon, obs_lat, observation_field, obs_radius, batch_order, obs_value, obs_error
):
    fields_count, member_count, rows_tile, cols_tile = ensemble.shape
    lat_index = lax.axis_index("lat")
    lat_count = lax.axis_size("lat")
    grid_lon = cols_tile * lax.axis_size("lon")
    mesh_northing = rows_tile * lat_count
    row_global = (lat_index * rows_tile + jnp.arange(rows_tile, dtype=jnp.int32)).astype(
        jnp.float32
    )
    rotation_frequency = (2.0 * jnp.sin(math.pi * ((row_global + 0.5) / mesh_northing - 0.5)))[
        :, None
    ]
    ints = jnp.stack([obs_lon, obs_lat, observation_field, obs_radius])[:, batch_order]
    floats = jnp.stack([obs_value, obs_error])[:, batch_order]
    batches = [
        (ints[:, b * NB : (b + 1) * NB], floats[:, b * NB : (b + 1) * NB]) for b in range(BATCHES)
    ]
    state = ensemble
    for step_index in range(STEPS):
        state = march_prediction(state, rotation_frequency)

    (lon0, lat0, kind0, radius0), (value0, error0) = batches[0]
    values, owned = at_owner(state, lon0, lat0, kind0)
    priors = lax.psum(jnp.where(owned[:, None], values, 0.0), ("lon", "lat"))
    for batch_index in range(BATCHES):
        (lon_b, lat_b, kind_b, radius_b), (value_b, error_b) = batches[batch_index]
        gains, anomaly = statistics(priors, value_b, error_b, member_count)
        if batch_index + 1 < BATCHES:
            (lon_n, lat_n, kind_n, _), _ = batches[batch_index + 1]
            values, owned = at_owner(state, lon_n, lat_n, kind_n)
            deviation = values - jnp.mean(values, axis=1, keepdims=True)
            covariance = jnp.einsum(
                "om,jm->oj", anomaly, deviation, precision=lax.Precision.HIGHEST
            ) / (member_count - 1)
            weights = localize(lon_n, lat_n, lon_b, lat_b, radius_b, grid_lon)
            increment = jnp.einsum(
                "om,oj->jm", gains, covariance * weights, precision=lax.Precision.HIGHEST
            )
            next_priors = lax.psum(
                jnp.where(owned[:, None], values + increment, 0.0), ("lon", "lat")
            )
        state = update(state, gains, anomaly, tile_weights(state, lon_b, lat_b, radius_b))
        if batch_index + 1 < BATCHES:
            priors = next_priors
    return state.astype(jnp.bfloat16)


def solution(mesh):
    placed = (P(None, None, "lat", "lon"), P(), P(), P(), P(), P(), P(), P())
    return jax.shard_map(
        shards, mesh=mesh, in_specs=placed, out_specs=P(None, None, "lat", "lon"), check_vma=False
    )
```

```python
import math

import jax
import jax.numpy as jnp
from jax import lax
from jax.sharding import PartitionSpec as P

STEPS = 2
BATCHES = 2
NB = 256


RATE = 0.4
DEPTHS = (1.0, 0.6, 0.35)
COUPLE = ((1.0, 0.5, 0.25), (0.5, 1.0, 0.5), (0.25, 0.5, 1.0))


HALO = 4


def ring_pairs(size, step):
    return [(i, (i + step) % size) for i in range(size)]


def line_pairs(size, step):
    return [(i, i + step) for i in range(size) if 0 <= i + step < size]


def widened(state):
    lon_n = lax.axis_size("lon")
    lat_n = lax.axis_size("lat")
    left = lax.ppermute(state[..., -HALO:], "lon", ring_pairs(lon_n, 1))
    right = lax.ppermute(state[..., :HALO], "lon", ring_pairs(lon_n, -1))
    wide = jnp.concatenate([left, state, right], axis=3)
    counts = (3, 3, 4)
    last = jnp.concatenate(
        [wide[3 * k : 3 * k + 3, :, -n:] for k, n in enumerate(counts)], axis=2
    )
    first = jnp.concatenate(
        [wide[3 * k : 3 * k + 3, :, :n] for k, n in enumerate(counts)], axis=2
    )
    before = lax.ppermute(last, "lat", line_pairs(lat_n, 1))
    after = lax.ppermute(first, "lat", line_pairs(lat_n, -1))
    parts = []
    offset = 0
    for k, n in enumerate(counts):
        block = wide[3 * k : 3 * k + 3]
        pad = jnp.zeros(block.shape[:2] + (HALO - n, block.shape[3]), block.dtype)
        parts.append(
            jnp.concatenate(
                [pad, before[:, :, offset : offset + n], block, after[:, :, offset : offset + n], pad],
                axis=2,
            )
        )
        offset += n
    return jnp.concatenate(parts)


def zonal(values):
    following = jnp.concatenate([values[..., 1:], values[..., -1:]], axis=3)
    preceding = jnp.concatenate([values[..., :1], values[..., :-1]], axis=3)
    return 0.5 * (following - preceding)


def meridional(values):
    following = jnp.concatenate([values[:, :, 1:, :], values[:, :, -1:, :]], axis=2)
    preceding = jnp.concatenate([values[:, :, :1, :], values[:, :, :-1, :]], axis=2)
    return 0.5 * (following - preceding)


def couple(height):
    return jnp.stack(
        [
            COUPLE[k][0] * height[0] + COUPLE[k][1] * height[1] + COUPLE[k][2] * height[2]
            for k in range(3)
        ]
    )


def march_prediction(running_member_set, rotation_frequency, inside):
    height = running_member_set[0:3]
    eastward_speed = running_member_set[3:6]
    merid_vel = running_member_set[6:9]
    depths = jnp.array(DEPTHS, jnp.float32)[:, None, None, None]
    height = height - RATE * depths * (zonal(eastward_speed) + meridional(merid_vel))
    height = jnp.where(inside, height, 0.0)
    pressure = couple(height)
    eastward_speed = (
        eastward_speed + RATE * rotation_frequency * merid_vel - RATE * zonal(pressure)
    )
    merid_vel = (
        merid_vel - RATE * rotation_frequency * eastward_speed - RATE * meridional(pressure)
    )
    merid_vel = jnp.where(inside, merid_vel, 0.0)
    return jnp.concatenate([height, eastward_speed, merid_vel])


def statistics(priors, values, errors, member_count):
    mean_obs = jnp.mean(priors, axis=1, keepdims=True)
    anomaly = priors - mean_obs
    variance = jnp.sum(anomaly * anomaly, axis=1, keepdims=True) / (member_count - 1)
    obs_err = errors[:, None]
    denominator = variance + obs_err
    shrink = 1.0 / (1.0 + jnp.sqrt(obs_err / denominator))
    gains = (values[:, None] - mean_obs - shrink * anomaly) / denominator
    return (gains, anomaly)


def localize(cell_lon, cell_lat, lon_obs, lat_obs, radius_obs, grid_lon):
    lon_gap = (cell_lon[None, :] - lon_obs[:, None]) % grid_lon
    lon_gap = jnp.minimum(lon_gap, grid_lon - lon_gap)
    lat_gap = cell_lat[None, :] - lat_obs[:, None]
    distance_sq = (lon_gap * lon_gap + lat_gap * lat_gap).astype(jnp.float32)
    radius_sq = (radius_obs * radius_obs).astype(jnp.float32)[:, None]
    return jnp.square(jnp.maximum(1.0 - distance_sq / radius_sq, 0.0))


def neighbourhood_sum(table):
    lon_n = lax.axis_size("lon")
    lat_n = lax.axis_size("lat")
    row = (
        table
        + lax.ppermute(table, "lon", ring_pairs(lon_n, 1))
        + lax.ppermute(table, "lon", ring_pairs(lon_n, -1))
    )
    return (
        row
        + lax.ppermute(row, "lat", line_pairs(lat_n, 1))
        + lax.ppermute(row, "lat", line_pairs(lat_n, -1))
    )


def tile_origin(state):
    _, _, rows_tile, cols_tile = state.shape
    return lax.axis_index("lon") * cols_tile, lax.axis_index("lat") * rows_tile


def at_owner(state, lon_obs, lat_obs, kind_obs):
    _, _, rows_tile, cols_tile = state.shape
    lon_base, lat_base = tile_origin(state)
    owned = (
        (lon_obs >= lon_base)
        & (lon_obs < lon_base + cols_tile)
        & (lat_obs >= lat_base)
        & (lat_obs < lat_base + rows_tile)
    )
    nearby_latitude = jnp.clip(lat_obs - lat_base, 0, rows_tile - 1)
    local_lon = jnp.clip(lon_obs - lon_base, 0, cols_tile - 1)
    values = state[kind_obs, :, nearby_latitude, local_lon]
    return values, owned


def update(state, gains, anomaly, weights):
    fields_count, member_count, rows_tile, cols_tile = state.shape
    flattened = state.reshape(fields_count, member_count, rows_tile * cols_tile)
    deviation = flattened - jnp.mean(flattened, axis=1, keepdims=True)
    covariance = jnp.einsum(
        "om,fmc->foc", anomaly, deviation, precision=lax.Precision.HIGHEST
    ) / (member_count - 1)
    increment = jnp.einsum(
        "om,foc->fmc", gains, covariance * weights[None], precision=lax.Precision.HIGHEST
    )
    return (flattened + increment).reshape(state.shape)


def tile_weights(state, lon_obs, lat_obs, radius_obs):
    _, _, rows_tile, cols_tile = state.shape
    lon_base, lat_base = tile_origin(state)
    grid_lon = cols_tile * lax.axis_size("lon")
    cell_lat = lat_base + jnp.repeat(jnp.arange(rows_tile, dtype=jnp.int32), cols_tile)
    cell_lon = lon_base + jnp.tile(jnp.arange(cols_tile, dtype=jnp.int32), rows_tile)
    return localize(cell_lon, cell_lat, lon_obs, lat_obs, radius_obs, grid_lon)


def shards(
    ensemble, obs_lon, obs_lat, observation_field, obs_radius, batch_order, obs_value, obs_error
):
    fields_count, member_count, rows_tile, cols_tile = ensemble.shape
    lat_index = lax.axis_index("lat")
    lat_count = lax.axis_size("lat")
    grid_lon = cols_tile * lax.axis_size("lon")
    mesh_northing = rows_tile * lat_count
    row_index = lat_index * rows_tile - HALO + jnp.arange(rows_tile + 2 * HALO, dtype=jnp.int32)
    inside = ((row_index >= 0) & (row_index < mesh_northing))[:, None]
    row_global = row_index.astype(jnp.float32)
    rotation_frequency = (2.0 * jnp.sin(math.pi * ((row_global + 0.5) / mesh_northing - 0.5)))[
        :, None
    ]
    ints = jnp.stack([obs_lon, obs_lat, observation_field, obs_radius])[:, batch_order]
    floats = jnp.stack([obs_value, obs_error])[:, batch_order]
    batches = [
        (ints[:, b * NB : (b + 1) * NB], floats[:, b * NB : (b + 1) * NB]) for b in range(BATCHES)
    ]
    state = widened(ensemble)
    for step_index in range(STEPS):
        state = march_prediction(state, rotation_frequency, inside)
    state = state[:, :, HALO : HALO + rows_tile, HALO : HALO + cols_tile]

    (lon0, lat0, kind0, radius0), (value0, error0) = batches[0]
    values, owned = at_owner(state, lon0, lat0, kind0)
    priors = neighbourhood_sum(jnp.where(owned[:, None], values, 0.0))
    for batch_index in range(BATCHES):
        (lon_b, lat_b, kind_b, radius_b), (value_b, error_b) = batches[batch_index]
        gains, anomaly = statistics(priors, value_b, error_b, member_count)
        if batch_index + 1 < BATCHES:
            (lon_n, lat_n, kind_n, _), _ = batches[batch_index + 1]
            values, owned = at_owner(state, lon_n, lat_n, kind_n)
            deviation = values - jnp.mean(values, axis=1, keepdims=True)
            covariance = jnp.einsum(
                "om,jm->oj", anomaly, deviation, precision=lax.Precision.HIGHEST
            ) / (member_count - 1)
            weights = localize(lon_n, lat_n, lon_b, lat_b, radius_b, grid_lon)
            increment = jnp.einsum(
                "om,oj->jm", gains, covariance * weights, precision=lax.Precision.HIGHEST
            )
            next_priors = neighbourhood_sum(jnp.where(owned[:, None], values + increment, 0.0))
        state = update(state, gains, anomaly, tile_weights(state, lon_b, lat_b, radius_b))
        if batch_index + 1 < BATCHES:
            priors = next_priors
    return state.astype(jnp.bfloat16)


def solution(mesh):
    placed = (P(None, None, "lat", "lon"), P(), P(), P(), P(), P(), P(), P())
    return jax.shard_map(
        shards, mesh=mesh, in_specs=placed, out_specs=P(None, None, "lat", "lon"), check_vma=False
    )
```

```python
import math

import jax
import jax.numpy as jnp
from jax import lax
from jax.sharding import PartitionSpec as P

STEPS = 2
BATCHES = 2
NB = 256


RATE = 0.4
DEPTHS = (1.0, 0.6, 0.35)
COUPLE = ((1.0, 0.5, 0.25), (0.5, 1.0, 0.5), (0.25, 0.5, 1.0))


def ring_pairs(size, step):
    return [(i, (i + step) % size) for i in range(size)]


def line_pairs(size, step):
    return [(i, i + step) for i in range(size) if 0 <= i + step < size]


def lon_edges(array):
    size = lax.axis_size("lon")
    up = [(i, (i + 1) % size) for i in range(size)]
    down = [((i + 1) % size, i) for i in range(size)]
    left = lax.ppermute(array[..., -1:], "lon", up)
    right = lax.ppermute(array[..., :1], "lon", down)
    return left, right


def lat_edges(array):
    size = lax.axis_size("lat")
    up = [(i, i + 1) for i in range(size - 1)]
    down = [(i + 1, i) for i in range(size - 1)]
    before = lax.ppermute(array[:, :, -1:, :], "lat", up)
    after = lax.ppermute(array[:, :, :1, :], "lat", down)
    return before, after


def zonal(values, left, right):
    following = jnp.concatenate([values[..., 1:], right], axis=3)
    preceding = jnp.concatenate([left, values[..., :-1]], axis=3)
    return 0.5 * (following - preceding)


def meridional(values, before, after):
    following = jnp.concatenate([values[:, :, 1:, :], after], axis=2)
    preceding = jnp.concatenate([before, values[:, :, :-1, :]], axis=2)
    return 0.5 * (following - preceding)


def couple(height):
    return jnp.stack(
        [
            COUPLE[k][0] * height[0] + COUPLE[k][1] * height[1] + COUPLE[k][2] * height[2]
            for k in range(3)
        ]
    )


def march_prediction(running_member_set, rotation_frequency):
    height = running_member_set[0:3]
    eastward_speed = running_member_set[3:6]
    merid_vel = running_member_set[6:9]
    depths = jnp.array(DEPTHS, jnp.float32)[:, None, None, None]
    u_left, u_right = lon_edges(eastward_speed)
    v_before, v_after = lat_edges(merid_vel)
    height = height - RATE * depths * (
        zonal(eastward_speed, u_left, u_right) + meridional(merid_vel, v_before, v_after)
    )
    pressure = couple(height)
    p_left, p_right = lon_edges(pressure)
    p_before, p_after = lat_edges(pressure)
    eastward_speed = (
        eastward_speed
        + RATE * rotation_frequency * merid_vel
        - RATE * zonal(pressure, p_left, p_right)
    )
    merid_vel = (
        merid_vel
        - RATE * rotation_frequency * eastward_speed
        - RATE * meridional(pressure, p_before, p_after)
    )
    return jnp.concatenate([height, eastward_speed, merid_vel])


def statistics(priors, values, errors, member_count):
    mean_obs = jnp.mean(priors, axis=1, keepdims=True)
    anomaly = priors - mean_obs
    variance = jnp.sum(anomaly * anomaly, axis=1, keepdims=True) / (member_count - 1)
    obs_err = errors[:, None]
    denominator = variance + obs_err
    shrink = 1.0 / (1.0 + jnp.sqrt(obs_err / denominator))
    gains = (values[:, None] - mean_obs - shrink * anomaly) / denominator
    return (gains, anomaly)


def localize(cell_lon, cell_lat, lon_obs, lat_obs, radius_obs, grid_lon):
    lon_gap = (cell_lon[None, :] - lon_obs[:, None]) % grid_lon
    lon_gap = jnp.minimum(lon_gap, grid_lon - lon_gap)
    lat_gap = cell_lat[None, :] - lat_obs[:, None]
    distance_sq = (lon_gap * lon_gap + lat_gap * lat_gap).astype(jnp.float32)
    radius_sq = (radius_obs * radius_obs).astype(jnp.float32)[:, None]
    return jnp.square(jnp.maximum(1.0 - distance_sq / radius_sq, 0.0))


def neighbourhood_sum(table):
    lon_n = lax.axis_size("lon")
    lat_n = lax.axis_size("lat")
    row = (
        table
        + lax.ppermute(table, "lon", ring_pairs(lon_n, 1))
        + lax.ppermute(table, "lon", ring_pairs(lon_n, -1))
    )
    return (
        row
        + lax.ppermute(row, "lat", line_pairs(lat_n, 1))
        + lax.ppermute(row, "lat", line_pairs(lat_n, -1))
    )


def tile_origin(state):
    _, _, rows_tile, cols_tile = state.shape
    return lax.axis_index("lon") * cols_tile, lax.axis_index("lat") * rows_tile


def at_owner(state, lon_obs, lat_obs, kind_obs):
    _, _, rows_tile, cols_tile = state.shape
    lon_base, lat_base = tile_origin(state)
    owned = (
        (lon_obs >= lon_base)
        & (lon_obs < lon_base + cols_tile)
        & (lat_obs >= lat_base)
        & (lat_obs < lat_base + rows_tile)
    )
    nearby_latitude = jnp.clip(lat_obs - lat_base, 0, rows_tile - 1)
    local_lon = jnp.clip(lon_obs - lon_base, 0, cols_tile - 1)
    values = state[kind_obs, :, nearby_latitude, local_lon]
    return values, owned


def update(state, gains, anomaly, weights):
    return jnp.concatenate(
        [update_group(state[f : f + 3], gains, anomaly, weights) for f in range(0, state.shape[0], 3)]
    )


def update_group(state, gains, anomaly, weights):
    fields_count, member_count, rows_tile, cols_tile = state.shape
    flattened = state.reshape(fields_count, member_count, rows_tile * cols_tile)
    deviation = flattened - jnp.mean(flattened, axis=1, keepdims=True)
    covariance = jnp.einsum(
        "om,fmc->foc", anomaly, deviation, precision=lax.Precision.HIGHEST
    ) / (member_count - 1)
    increment = jnp.einsum(
        "om,foc->fmc", gains, covariance * weights[None], precision=lax.Precision.HIGHEST
    )
    return (flattened + increment).reshape(state.shape)


def tile_weights(state, lon_obs, lat_obs, radius_obs):
    _, _, rows_tile, cols_tile = state.shape
    lon_base, lat_base = tile_origin(state)
    grid_lon = cols_tile * lax.axis_size("lon")
    cell_lat = lat_base + jnp.repeat(jnp.arange(rows_tile, dtype=jnp.int32), cols_tile)
    cell_lon = lon_base + jnp.tile(jnp.arange(cols_tile, dtype=jnp.int32), rows_tile)
    return localize(cell_lon, cell_lat, lon_obs, lat_obs, radius_obs, grid_lon)


def shards(
    ensemble, obs_lon, obs_lat, observation_field, obs_radius, batch_order, obs_value, obs_error
):
    fields_count, member_count, rows_tile, cols_tile = ensemble.shape
    lat_index = lax.axis_index("lat")
    lat_count = lax.axis_size("lat")
    lon_size = lax.axis_size("lon")
    lat_size = lax.axis_size("lat")
    grid_lon = cols_tile * lon_size
    mesh_northing = rows_tile * lat_count
    row_global = (lat_index * rows_tile + jnp.arange(rows_tile, dtype=jnp.int32)).astype(
        jnp.float32
    )
    rotation_frequency = (2.0 * jnp.sin(math.pi * ((row_global + 0.5) / mesh_northing - 0.5)))[
        :, None
    ]
    ints = jnp.stack([obs_lon, obs_lat, observation_field, obs_radius])[:, batch_order]
    floats = jnp.stack([obs_value, obs_error])[:, batch_order]
    batches = [
        (ints[:, b * NB : (b + 1) * NB], floats[:, b * NB : (b + 1) * NB]) for b in range(BATCHES)
    ]
    state = ensemble
    for step_index in range(STEPS):
        state = march_prediction(state, rotation_frequency)

    (lon0, lat0, kind0, radius0), (value0, error0) = batches[0]
    values, owned = at_owner(state, lon0, lat0, kind0)
    priors = neighbourhood_sum(jnp.where(owned[:, None], values, 0.0))
    for batch_index in range(BATCHES):
        (lon_b, lat_b, kind_b, radius_b), (value_b, error_b) = batches[batch_index]
        gains, anomaly = statistics(priors, value_b, error_b, member_count)
        if batch_index + 1 < BATCHES:
            (lon_n, lat_n, kind_n, _), _ = batches[batch_index + 1]
            values, owned = at_owner(state, lon_n, lat_n, kind_n)
            deviation = values - jnp.mean(values, axis=1, keepdims=True)
            covariance = jnp.einsum(
                "om,jm->oj", anomaly, deviation, precision=lax.Precision.HIGHEST
            ) / (member_count - 1)
            weights = localize(lon_n, lat_n, lon_b, lat_b, radius_b, grid_lon)
            increment = jnp.einsum(
                "om,oj->jm", gains, covariance * weights, precision=lax.Precision.HIGHEST
            )
            table = jnp.where(owned[:, None], values + increment, 0.0)
            weights = tile_weights(state, lon_b, lat_b, radius_b)
            table, head = lax.optimization_barrier((table, state[0:3]))
            row = (
                table
                + lax.ppermute(table, "lon", ring_pairs(lon_size, 1))
                + lax.ppermute(table, "lon", ring_pairs(lon_size, -1))
            )
            head = update(head, gains, anomaly, weights)
            row, tail, head = lax.optimization_barrier((row, state[3:], head))
            priors = (
                row
                + lax.ppermute(row, "lat", line_pairs(lat_size, 1))
                + lax.ppermute(row, "lat", line_pairs(lat_size, -1))
            )
            state = jnp.concatenate([head, update(tail, gains, anomaly, weights)])
        else:
            state = update(state, gains, anomaly, tile_weights(state, lon_b, lat_b, radius_b))
    return state.astype(jnp.bfloat16)


def solution(mesh):
    placed = (P(None, None, "lat", "lon"), P(), P(), P(), P(), P(), P(), P())
    return jax.shard_map(
        shards, mesh=mesh, in_specs=placed, out_specs=P(None, None, "lat", "lon"), check_vma=False
    )
```

```python
import math

import jax
import jax.numpy as jnp
from jax import lax
from jax.sharding import PartitionSpec as P

STEPS = 2
BATCHES = 2
NB = 256


RATE = 0.4
DEPTHS = (1.0, 0.6, 0.35)
COUPLE = ((1.0, 0.5, 0.25), (0.5, 1.0, 0.5), (0.25, 0.5, 1.0))


def ring_pairs(size, step):
    return [(i, (i + step) % size) for i in range(size)]


def line_pairs(size, step):
    return [(i, i + step) for i in range(size) if 0 <= i + step < size]


def lon_edges(array):
    size = lax.axis_size("lon")
    up = [(i, (i + 1) % size) for i in range(size)]
    down = [((i + 1) % size, i) for i in range(size)]
    left = lax.ppermute(array[..., -1:], "lon", up)
    right = lax.ppermute(array[..., :1], "lon", down)
    return left, right


def lat_edges(array):
    size = lax.axis_size("lat")
    up = [(i, i + 1) for i in range(size - 1)]
    down = [(i + 1, i) for i in range(size - 1)]
    before = lax.ppermute(array[:, :, -1:, :], "lat", up)
    after = lax.ppermute(array[:, :, :1, :], "lat", down)
    return before, after


def zonal(values, left, right):
    following = jnp.concatenate([values[..., 1:], right], axis=3)
    preceding = jnp.concatenate([left, values[..., :-1]], axis=3)
    return 0.5 * (following - preceding)


def meridional(values, before, after):
    following = jnp.concatenate([values[:, :, 1:, :], after], axis=2)
    preceding = jnp.concatenate([before, values[:, :, :-1, :]], axis=2)
    return 0.5 * (following - preceding)


def couple(height):
    return jnp.stack(
        [
            COUPLE[k][0] * height[0] + COUPLE[k][1] * height[1] + COUPLE[k][2] * height[2]
            for k in range(3)
        ]
    )


def march_prediction(running_member_set, rotation_frequency):
    height = running_member_set[0:3]
    eastward_speed = running_member_set[3:6]
    merid_vel = running_member_set[6:9]
    depths = jnp.array(DEPTHS, jnp.float32)[:, None, None, None]
    u_left, u_right = lon_edges(eastward_speed)
    v_before, v_after = lat_edges(merid_vel)
    height = height - RATE * depths * (
        zonal(eastward_speed, u_left, u_right) + meridional(merid_vel, v_before, v_after)
    )
    pressure = couple(height)
    p_left, p_right = lon_edges(pressure)
    p_before, p_after = lat_edges(pressure)
    eastward_speed = (
        eastward_speed
        + RATE * rotation_frequency * merid_vel
        - RATE * zonal(pressure, p_left, p_right)
    )
    merid_vel = (
        merid_vel
        - RATE * rotation_frequency * eastward_speed
        - RATE * meridional(pressure, p_before, p_after)
    )
    return jnp.concatenate([height, eastward_speed, merid_vel])


def statistics(priors, values, errors, member_count):
    mean_obs = jnp.mean(priors, axis=1, keepdims=True)
    anomaly = priors - mean_obs
    variance = jnp.sum(anomaly * anomaly, axis=1, keepdims=True) / (member_count - 1)
    obs_err = errors[:, None]
    denominator = variance + obs_err
    shrink = 1.0 / (1.0 + jnp.sqrt(obs_err / denominator))
    gains = (values[:, None] - mean_obs - shrink * anomaly) / denominator
    return (gains, anomaly)


def localize(cell_lon, cell_lat, lon_obs, lat_obs, radius_obs, grid_lon):
    lon_gap = (cell_lon[None, :] - lon_obs[:, None]) % grid_lon
    lon_gap = jnp.minimum(lon_gap, grid_lon - lon_gap)
    lat_gap = cell_lat[None, :] - lat_obs[:, None]
    distance_sq = (lon_gap * lon_gap + lat_gap * lat_gap).astype(jnp.float32)
    radius_sq = (radius_obs * radius_obs).astype(jnp.float32)[:, None]
    return jnp.square(jnp.maximum(1.0 - distance_sq / radius_sq, 0.0))


def neighbourhood_sum(table):
    lon_n = lax.axis_size("lon")
    lat_n = lax.axis_size("lat")
    row = (
        table
        + lax.ppermute(table, "lon", ring_pairs(lon_n, 1))
        + lax.ppermute(table, "lon", ring_pairs(lon_n, -1))
    )
    return (
        row
        + lax.ppermute(row, "lat", line_pairs(lat_n, 1))
        + lax.ppermute(row, "lat", line_pairs(lat_n, -1))
    )


def tile_origin(state):
    _, _, rows_tile, cols_tile = state.shape
    return lax.axis_index("lon") * cols_tile, lax.axis_index("lat") * rows_tile


def at_owner(state, lon_obs, lat_obs, kind_obs):
    _, _, rows_tile, cols_tile = state.shape
    lon_base, lat_base = tile_origin(state)
    owned = (
        (lon_obs >= lon_base)
        & (lon_obs < lon_base + cols_tile)
        & (lat_obs >= lat_base)
        & (lat_obs < lat_base + rows_tile)
    )
    nearby_latitude = jnp.clip(lat_obs - lat_base, 0, rows_tile - 1)
    local_lon = jnp.clip(lon_obs - lon_base, 0, cols_tile - 1)
    rows = state[kind_obs, :, nearby_latitude, :]
    pick = jnp.arange(cols_tile, dtype=jnp.int32)[None, :] == local_lon[:, None]
    values = jnp.sum(jnp.where(pick[:, None, :], rows, 0.0), axis=2)
    return values, owned


def update(state, gains, anomaly, weights):
    return jnp.concatenate(
        [update_group(state[f : f + 3], gains, anomaly, weights) for f in range(0, state.shape[0], 3)]
    )


def update_group(state, gains, anomaly, weights):
    fields_count, member_count, rows_tile, cols_tile = state.shape
    flattened = state.reshape(fields_count, member_count, rows_tile * cols_tile)
    deviation = flattened - jnp.mean(flattened, axis=1, keepdims=True)
    covariance = jnp.einsum(
        "om,fmc->foc", anomaly, deviation, precision=lax.Precision.HIGH
    ) / (member_count - 1)
    increment = jnp.einsum(
        "om,foc->fmc", gains, covariance * weights[None], precision=lax.Precision.HIGH
    )
    return (flattened + increment).reshape(state.shape)


def tile_weights(state, lon_obs, lat_obs, radius_obs):
    _, _, rows_tile, cols_tile = state.shape
    lon_base, lat_base = tile_origin(state)
    grid_lon = cols_tile * lax.axis_size("lon")
    cell_lat = lat_base + jnp.repeat(jnp.arange(rows_tile, dtype=jnp.int32), cols_tile)
    cell_lon = lon_base + jnp.tile(jnp.arange(cols_tile, dtype=jnp.int32), rows_tile)
    return localize(cell_lon, cell_lat, lon_obs, lat_obs, radius_obs, grid_lon)


def shards(
    ensemble, obs_lon, obs_lat, observation_field, obs_radius, batch_order, obs_value, obs_error
):
    fields_count, member_count, rows_tile, cols_tile = ensemble.shape
    lat_index = lax.axis_index("lat")
    lat_count = lax.axis_size("lat")
    lon_size = lax.axis_size("lon")
    lat_size = lax.axis_size("lat")
    grid_lon = cols_tile * lon_size
    mesh_northing = rows_tile * lat_count
    row_global = (lat_index * rows_tile + jnp.arange(rows_tile, dtype=jnp.int32)).astype(
        jnp.float32
    )
    rotation_frequency = (2.0 * jnp.sin(math.pi * ((row_global + 0.5) / mesh_northing - 0.5)))[
        :, None
    ]
    ints = jnp.stack([obs_lon, obs_lat, observation_field, obs_radius])[:, batch_order]
    floats = jnp.stack([obs_value, obs_error])[:, batch_order]
    batches = [
        (ints[:, b * NB : (b + 1) * NB], floats[:, b * NB : (b + 1) * NB]) for b in range(BATCHES)
    ]
    state = ensemble
    for step_index in range(STEPS):
        state = march_prediction(state, rotation_frequency)

    (lon0, lat0, kind0, radius0), (value0, error0) = batches[0]
    values, owned = at_owner(state, lon0, lat0, kind0)
    priors = neighbourhood_sum(jnp.where(owned[:, None], values, 0.0))
    for batch_index in range(BATCHES):
        (lon_b, lat_b, kind_b, radius_b), (value_b, error_b) = batches[batch_index]
        gains, anomaly = statistics(priors, value_b, error_b, member_count)
        if batch_index + 1 < BATCHES:
            (lon_n, lat_n, kind_n, _), _ = batches[batch_index + 1]
            values, owned = at_owner(state, lon_n, lat_n, kind_n)
            deviation = values - jnp.mean(values, axis=1, keepdims=True)
            covariance = jnp.einsum(
                "om,jm->oj", anomaly, deviation, precision=lax.Precision.HIGH
            ) / (member_count - 1)
            weights = localize(lon_n, lat_n, lon_b, lat_b, radius_b, grid_lon)
            increment = jnp.einsum(
                "om,oj->jm", gains, covariance * weights, precision=lax.Precision.HIGH
            )
            table = jnp.where(owned[:, None], values + increment, 0.0)
            weights = tile_weights(state, lon_b, lat_b, radius_b)
            table, head = lax.optimization_barrier((table, state[0:3]))
            row = (
                table
                + lax.ppermute(table, "lon", ring_pairs(lon_size, 1))
                + lax.ppermute(table, "lon", ring_pairs(lon_size, -1))
            )
            head = update(head, gains, anomaly, weights)
            row, tail, head = lax.optimization_barrier((row, state[3:], head))
            priors = (
                row
                + lax.ppermute(row, "lat", line_pairs(lat_size, 1))
                + lax.ppermute(row, "lat", line_pairs(lat_size, -1))
            )
            state = jnp.concatenate([head, update(tail, gains, anomaly, weights)])
        else:
            state = update(state, gains, anomaly, tile_weights(state, lon_b, lat_b, radius_b))
    return state.astype(jnp.bfloat16)


def solution(mesh):
    placed = (P(None, None, "lat", "lon"), P(), P(), P(), P(), P(), P(), P())
    return jax.shard_map(
        shards, mesh=mesh, in_specs=placed, out_specs=P(None, None, "lat", "lon"), check_vma=False
    )
```

```python
import math

import jax
import jax.numpy as jnp
from jax import lax
from jax.sharding import PartitionSpec as P

STEPS = 2
BATCHES = 2
NB = 256


RATE = 0.4
DEPTHS = (1.0, 0.6, 0.35)
COUPLE = ((1.0, 0.5, 0.25), (0.5, 1.0, 0.5), (0.25, 0.5, 1.0))


def ring_pairs(size, step):
    return [(i, (i + step) % size) for i in range(size)]


def line_pairs(size, step):
    return [(i, i + step) for i in range(size) if 0 <= i + step < size]


def lon_edges(array):
    size = lax.axis_size("lon")
    up = [(i, (i + 1) % size) for i in range(size)]
    down = [((i + 1) % size, i) for i in range(size)]
    left = lax.ppermute(array[..., -1:], "lon", up)
    right = lax.ppermute(array[..., :1], "lon", down)
    return left, right


def lat_edges(array):
    size = lax.axis_size("lat")
    up = [(i, i + 1) for i in range(size - 1)]
    down = [(i + 1, i) for i in range(size - 1)]
    before = lax.ppermute(array[:, :, -1:, :], "lat", up)
    after = lax.ppermute(array[:, :, :1, :], "lat", down)
    return before, after


def zonal(values, left, right):
    following = jnp.concatenate([values[..., 1:], right], axis=3)
    preceding = jnp.concatenate([left, values[..., :-1]], axis=3)
    return 0.5 * (following - preceding)


def meridional(values, before, after):
    following = jnp.concatenate([values[:, :, 1:, :], after], axis=2)
    preceding = jnp.concatenate([before, values[:, :, :-1, :]], axis=2)
    return 0.5 * (following - preceding)


def couple(height):
    return jnp.stack(
        [
            COUPLE[k][0] * height[0] + COUPLE[k][1] * height[1] + COUPLE[k][2] * height[2]
            for k in range(3)
        ]
    )


def march_prediction(running_member_set, rotation_frequency):
    height = running_member_set[0:3]
    eastward_speed = running_member_set[3:6]
    merid_vel = running_member_set[6:9]
    depths = jnp.array(DEPTHS, jnp.float32)[:, None, None, None]
    u_left, u_right = lon_edges(eastward_speed)
    v_before, v_after = lat_edges(merid_vel)
    height = height - RATE * depths * (
        zonal(eastward_speed, u_left, u_right) + meridional(merid_vel, v_before, v_after)
    )
    pressure = couple(height)
    p_left, p_right = lon_edges(pressure)
    p_before, p_after = lat_edges(pressure)
    eastward_speed = (
        eastward_speed
        + RATE * rotation_frequency * merid_vel
        - RATE * zonal(pressure, p_left, p_right)
    )
    merid_vel = (
        merid_vel
        - RATE * rotation_frequency * eastward_speed
        - RATE * meridional(pressure, p_before, p_after)
    )
    return jnp.concatenate([height, eastward_speed, merid_vel])


def statistics(priors, values, errors, member_count):
    mean_obs = jnp.mean(priors, axis=1, keepdims=True)
    anomaly = priors - mean_obs
    variance = jnp.sum(anomaly * anomaly, axis=1, keepdims=True) / (member_count - 1)
    obs_err = errors[:, None]
    denominator = variance + obs_err
    shrink = 1.0 / (1.0 + jnp.sqrt(obs_err / denominator))
    gains = (values[:, None] - mean_obs - shrink * anomaly) / denominator
    return (gains, anomaly)


def localize(cell_lon, cell_lat, lon_obs, lat_obs, radius_obs, grid_lon):
    lon_gap = (cell_lon[None, :] - lon_obs[:, None]) % grid_lon
    lon_gap = jnp.minimum(lon_gap, grid_lon - lon_gap)
    lat_gap = cell_lat[None, :] - lat_obs[:, None]
    distance_sq = (lon_gap * lon_gap + lat_gap * lat_gap).astype(jnp.float32)
    radius_sq = (radius_obs * radius_obs).astype(jnp.float32)[:, None]
    return jnp.square(jnp.maximum(1.0 - distance_sq / radius_sq, 0.0))


def neighbourhood_sum(table):
    lon_n = lax.axis_size("lon")
    lat_n = lax.axis_size("lat")
    row = (
        table
        + lax.ppermute(table, "lon", ring_pairs(lon_n, 1))
        + lax.ppermute(table, "lon", ring_pairs(lon_n, -1))
    )
    return (
        row
        + lax.ppermute(row, "lat", line_pairs(lat_n, 1))
        + lax.ppermute(row, "lat", line_pairs(lat_n, -1))
    )


def tile_origin(state):
    _, _, rows_tile, cols_tile = state.shape
    return lax.axis_index("lon") * cols_tile, lax.axis_index("lat") * rows_tile


def at_owner(state, lon_obs, lat_obs, kind_obs):
    _, _, rows_tile, cols_tile = state.shape
    lon_base, lat_base = tile_origin(state)
    owned = (
        (lon_obs >= lon_base)
        & (lon_obs < lon_base + cols_tile)
        & (lat_obs >= lat_base)
        & (lat_obs < lat_base + rows_tile)
    )
    nearby_latitude = jnp.clip(lat_obs - lat_base, 0, rows_tile - 1)
    local_lon = jnp.clip(lon_obs - lon_base, 0, cols_tile - 1)
    rows = state[kind_obs, :, nearby_latitude, :]
    pick = jnp.arange(cols_tile, dtype=jnp.int32)[None, :] == local_lon[:, None]
    values = jnp.sum(jnp.where(pick[:, None, :], rows, 0.0), axis=2)
    return values, owned


def update(state, gains, anomaly, weights):
    return jnp.concatenate(
        [update_group(state[f : f + 3], gains, anomaly, weights) for f in range(0, state.shape[0], 3)]
    )


def update_group(state, gains, anomaly, weights):
    fields_count, member_count, rows_tile, cols_tile = state.shape
    flattened = state.reshape(fields_count, member_count, rows_tile * cols_tile)
    deviation = flattened - jnp.mean(flattened, axis=1, keepdims=True)
    covariance = jnp.einsum(
        "om,fmc->foc", anomaly, deviation, precision=lax.Precision.HIGH
    ) / (member_count - 1)
    increment = jnp.einsum(
        "om,foc->fmc", gains, covariance * weights[None], precision=lax.Precision.HIGH
    )
    return (flattened + increment).reshape(state.shape)


def tile_weights(state, lon_obs, lat_obs, radius_obs):
    _, _, rows_tile, cols_tile = state.shape
    lon_base, lat_base = tile_origin(state)
    grid_lon = cols_tile * lax.axis_size("lon")
    cell_lat = lat_base + jnp.repeat(jnp.arange(rows_tile, dtype=jnp.int32), cols_tile)
    cell_lon = lon_base + jnp.tile(jnp.arange(cols_tile, dtype=jnp.int32), rows_tile)
    return localize(cell_lon, cell_lat, lon_obs, lat_obs, radius_obs, grid_lon)


def shards(
    ensemble, obs_lon, obs_lat, observation_field, obs_radius, batch_order, obs_value, obs_error
):
    fields_count, member_count, rows_tile, cols_tile = ensemble.shape
    lat_index = lax.axis_index("lat")
    lat_count = lax.axis_size("lat")
    lon_size = lax.axis_size("lon")
    lat_size = lax.axis_size("lat")
    grid_lon = cols_tile * lon_size
    mesh_northing = rows_tile * lat_count
    row_global = (lat_index * rows_tile + jnp.arange(rows_tile, dtype=jnp.int32)).astype(
        jnp.float32
    )
    rotation_frequency = (2.0 * jnp.sin(math.pi * ((row_global + 0.5) / mesh_northing - 0.5)))[
        :, None
    ]
    ints = jnp.stack([obs_lon, obs_lat, observation_field, obs_radius])[:, batch_order]
    floats = jnp.stack([obs_value, obs_error])[:, batch_order]
    batches = [
        (ints[:, b * NB : (b + 1) * NB], floats[:, b * NB : (b + 1) * NB]) for b in range(BATCHES)
    ]
    state = ensemble
    for step_index in range(STEPS):
        state = march_prediction(state, rotation_frequency)

    (lon0, lat0, kind0, radius0), (value0, error0) = batches[0]
    (lon1, lat1, kind1, radius1), (value1, error1) = batches[1]
    values0, owned0 = at_owner(state, lon0, lat0, kind0)
    values1, owned1 = at_owner(state, lon1, lat1, kind1)
    table0 = jnp.where(owned0[:, None], values0, 0.0)
    table1 = jnp.where(owned1[:, None], values1, 0.0)
    both = jnp.concatenate([table0, table1])
    both = (
        both
        + lax.ppermute(both, "lon", ring_pairs(lon_size, 1))
        + lax.ppermute(both, "lon", ring_pairs(lon_size, -1))
    )
    wide0 = (
        both[:NB]
        + lax.ppermute(table0, "lon", ring_pairs(lon_size, 2))
        + lax.ppermute(table0, "lon", ring_pairs(lon_size, -2))
    )
    both = jnp.concatenate([wide0, both[NB:]])
    both = (
        both
        + lax.ppermute(both, "lat", line_pairs(lat_size, 1))
        + lax.ppermute(both, "lat", line_pairs(lat_size, -1))
    )
    priors = (
        both[:NB]
        + lax.ppermute(wide0, "lat", line_pairs(lat_size, 2))
        + lax.ppermute(wide0, "lat", line_pairs(lat_size, -2))
    )
    raw1 = both[NB:]
    gains, anomaly = statistics(priors, value0, error0, member_count)
    deviation = raw1 - jnp.mean(raw1, axis=1, keepdims=True)
    covariance = jnp.einsum(
        "om,jm->oj", anomaly, deviation, precision=lax.Precision.HIGH
    ) / (member_count - 1)
    weights = localize(lon1, lat1, lon0, lat0, radius0, grid_lon)
    increment = jnp.einsum("om,oj->jm", gains, covariance * weights, precision=lax.Precision.HIGH)
    priors1 = raw1 + increment
    state = update(state, gains, anomaly, tile_weights(state, lon0, lat0, radius0))
    gains, anomaly = statistics(priors1, value1, error1, member_count)
    state = update(state, gains, anomaly, tile_weights(state, lon1, lat1, radius1))
    return state.astype(jnp.bfloat16)


def solution(mesh):
    placed = (P(None, None, "lat", "lon"), P(), P(), P(), P(), P(), P(), P())
    return jax.shard_map(
        shards, mesh=mesh, in_specs=placed, out_specs=P(None, None, "lat", "lon"), check_vma=False
    )
```

```python
import math

import jax
import jax.numpy as jnp
from jax import lax
from jax.sharding import PartitionSpec as P

STEPS = 2
BATCHES = 2
NB = 256


RATE = 0.4
DEPTHS = (1.0, 0.6, 0.35)
COUPLE = ((1.0, 0.5, 0.25), (0.5, 1.0, 0.5), (0.25, 0.5, 1.0))


def ring_pairs(size, step):
    return [(i, (i + step) % size) for i in range(size)]


def line_pairs(size, step):
    return [(i, i + step) for i in range(size) if 0 <= i + step < size]


def lon_edges(array):
    size = lax.axis_size("lon")
    up = [(i, (i + 1) % size) for i in range(size)]
    down = [((i + 1) % size, i) for i in range(size)]
    left = lax.ppermute(array[..., -1:], "lon", up)
    right = lax.ppermute(array[..., :1], "lon", down)
    return left, right


def lat_edges(array):
    size = lax.axis_size("lat")
    up = [(i, i + 1) for i in range(size - 1)]
    down = [(i + 1, i) for i in range(size - 1)]
    before = lax.ppermute(array[:, :, -1:, :], "lat", up)
    after = lax.ppermute(array[:, :, :1, :], "lat", down)
    return before, after


def zonal(values, left, right):
    following = jnp.concatenate([values[..., 1:], right], axis=3)
    preceding = jnp.concatenate([left, values[..., :-1]], axis=3)
    return 0.5 * (following - preceding)


def meridional(values, before, after):
    following = jnp.concatenate([values[:, :, 1:, :], after], axis=2)
    preceding = jnp.concatenate([before, values[:, :, :-1, :]], axis=2)
    return 0.5 * (following - preceding)


def couple(height):
    return jnp.stack(
        [
            COUPLE[k][0] * height[0] + COUPLE[k][1] * height[1] + COUPLE[k][2] * height[2]
            for k in range(3)
        ]
    )


def march_prediction(running_member_set, rotation_frequency):
    height = running_member_set[0:3]
    eastward_speed = running_member_set[3:6]
    merid_vel = running_member_set[6:9]
    depths = jnp.array(DEPTHS, jnp.float32)[:, None, None, None]
    u_left, u_right = lon_edges(eastward_speed)
    v_before, v_after = lat_edges(merid_vel)
    height = height - RATE * depths * (
        zonal(eastward_speed, u_left, u_right) + meridional(merid_vel, v_before, v_after)
    )
    pressure = couple(height)
    p_left, p_right = lon_edges(pressure)
    p_before, p_after = lat_edges(pressure)
    eastward_speed = (
        eastward_speed
        + RATE * rotation_frequency * merid_vel
        - RATE * zonal(pressure, p_left, p_right)
    )
    merid_vel = (
        merid_vel
        - RATE * rotation_frequency * eastward_speed
        - RATE * meridional(pressure, p_before, p_after)
    )
    return jnp.concatenate([height, eastward_speed, merid_vel])


def statistics(priors, values, errors, member_count):
    mean_obs = jnp.mean(priors, axis=1, keepdims=True)
    anomaly = priors - mean_obs
    variance = jnp.sum(anomaly * anomaly, axis=1, keepdims=True) / (member_count - 1)
    obs_err = errors[:, None]
    denominator = variance + obs_err
    shrink = 1.0 / (1.0 + jnp.sqrt(obs_err / denominator))
    gains = (values[:, None] - mean_obs - shrink * anomaly) / denominator
    return (gains, anomaly)


def localize(cell_lon, cell_lat, lon_obs, lat_obs, radius_obs, grid_lon):
    lon_gap = (cell_lon[None, :] - lon_obs[:, None]) % grid_lon
    lon_gap = jnp.minimum(lon_gap, grid_lon - lon_gap)
    lat_gap = cell_lat[None, :] - lat_obs[:, None]
    distance_sq = (lon_gap * lon_gap + lat_gap * lat_gap).astype(jnp.float32)
    radius_sq = (radius_obs * radius_obs).astype(jnp.float32)[:, None]
    return jnp.square(jnp.maximum(1.0 - distance_sq / radius_sq, 0.0))


def neighbourhood_sum(table):
    lon_n = lax.axis_size("lon")
    lat_n = lax.axis_size("lat")
    row = (
        table
        + lax.ppermute(table, "lon", ring_pairs(lon_n, 1))
        + lax.ppermute(table, "lon", ring_pairs(lon_n, -1))
    )
    return (
        row
        + lax.ppermute(row, "lat", line_pairs(lat_n, 1))
        + lax.ppermute(row, "lat", line_pairs(lat_n, -1))
    )


def tile_origin(state):
    _, _, rows_tile, cols_tile = state.shape
    return lax.axis_index("lon") * cols_tile, lax.axis_index("lat") * rows_tile


def owner_table(state, lon_obs, lat_obs, kind_obs):
    fields_count, _, rows_tile, cols_tile = state.shape
    lon_base, lat_base = tile_origin(state)
    row_hit = jnp.arange(rows_tile, dtype=jnp.int32)[None, :] == (lat_obs - lat_base)[:, None]
    col_hit = jnp.arange(cols_tile, dtype=jnp.int32)[None, :] == (lon_obs - lon_base)[:, None]
    cell = (row_hit[:, :, None] & col_hit[:, None, :]).astype(jnp.float32)
    picked = jnp.einsum("jrc,fmrc->jfm", cell, state, precision=lax.Precision.HIGHEST)
    field_hit = jnp.arange(fields_count, dtype=jnp.int32)[None, :] == kind_obs[:, None]
    return jnp.sum(jnp.where(field_hit[:, :, None], picked, 0.0), axis=1)


def update(state, gains, anomaly, weights):
    return jnp.concatenate(
        [update_group(state[f : f + 3], gains, anomaly, weights) for f in range(0, state.shape[0], 3)]
    )


def update_group(state, gains, anomaly, weights):
    fields_count, member_count, rows_tile, cols_tile = state.shape
    flattened = state.reshape(fields_count, member_count, rows_tile * cols_tile)
    deviation = flattened - jnp.mean(flattened, axis=1, keepdims=True)
    covariance = jnp.einsum(
        "om,fmc->foc", anomaly, deviation, precision=lax.Precision.HIGH
    ) / (member_count - 1)
    increment = jnp.einsum(
        "om,foc->fmc", gains, covariance * weights[None], precision=lax.Precision.HIGH
    )
    return (flattened + increment).reshape(state.shape)


def tile_weights(state, lon_obs, lat_obs, radius_obs):
    _, _, rows_tile, cols_tile = state.shape
    lon_base, lat_base = tile_origin(state)
    grid_lon = cols_tile * lax.axis_size("lon")
    cell_lat = lat_base + jnp.repeat(jnp.arange(rows_tile, dtype=jnp.int32), cols_tile)
    cell_lon = lon_base + jnp.tile(jnp.arange(cols_tile, dtype=jnp.int32), rows_tile)
    return localize(cell_lon, cell_lat, lon_obs, lat_obs, radius_obs, grid_lon)


def shards(
    ensemble, obs_lon, obs_lat, observation_field, obs_radius, batch_order, obs_value, obs_error
):
    fields_count, member_count, rows_tile, cols_tile = ensemble.shape
    lat_index = lax.axis_index("lat")
    lat_count = lax.axis_size("lat")
    lon_size = lax.axis_size("lon")
    lat_size = lax.axis_size("lat")
    grid_lon = cols_tile * lon_size
    mesh_northing = rows_tile * lat_count
    row_global = (lat_index * rows_tile + jnp.arange(rows_tile, dtype=jnp.int32)).astype(
        jnp.float32
    )
    rotation_frequency = (2.0 * jnp.sin(math.pi * ((row_global + 0.5) / mesh_northing - 0.5)))[
        :, None
    ]
    ints = jnp.stack([obs_lon, obs_lat, observation_field, obs_radius])[:, batch_order]
    floats = jnp.stack([obs_value, obs_error])[:, batch_order]
    batches = [
        (ints[:, b * NB : (b + 1) * NB], floats[:, b * NB : (b + 1) * NB]) for b in range(BATCHES)
    ]
    state = ensemble
    for step_index in range(STEPS):
        state = march_prediction(state, rotation_frequency)

    (lon0, lat0, kind0, radius0), (value0, error0) = batches[0]
    (lon1, lat1, kind1, radius1), (value1, error1) = batches[1]
    table0, table1 = jnp.split(owner_table(state, ints[0], ints[1], ints[2]), 2)
    both = jnp.concatenate([table0, table1])
    both = (
        both
        + lax.ppermute(both, "lon", ring_pairs(lon_size, 1))
        + lax.ppermute(both, "lon", ring_pairs(lon_size, -1))
    )
    wide0 = (
        both[:NB]
        + lax.ppermute(table0, "lon", ring_pairs(lon_size, 2))
        + lax.ppermute(table0, "lon", ring_pairs(lon_size, -2))
    )
    both = jnp.concatenate([wide0, both[NB:]])
    both = (
        both
        + lax.ppermute(both, "lat", line_pairs(lat_size, 1))
        + lax.ppermute(both, "lat", line_pairs(lat_size, -1))
    )
    priors = (
        both[:NB]
        + lax.ppermute(wide0, "lat", line_pairs(lat_size, 2))
        + lax.ppermute(wide0, "lat", line_pairs(lat_size, -2))
    )
    raw1 = both[NB:]
    gains, anomaly = statistics(priors, value0, error0, member_count)
    deviation = raw1 - jnp.mean(raw1, axis=1, keepdims=True)
    covariance = jnp.einsum(
        "om,jm->oj", anomaly, deviation, precision=lax.Precision.HIGH
    ) / (member_count - 1)
    weights = localize(lon1, lat1, lon0, lat0, radius0, grid_lon)
    increment = jnp.einsum("om,oj->jm", gains, covariance * weights, precision=lax.Precision.HIGH)
    priors1 = raw1 + increment
    state = update(state, gains, anomaly, tile_weights(state, lon0, lat0, radius0))
    gains, anomaly = statistics(priors1, value1, error1, member_count)
    state = update(state, gains, anomaly, tile_weights(state, lon1, lat1, radius1))
    return state.astype(jnp.bfloat16)


def solution(mesh):
    placed = (P(None, None, "lat", "lon"), P(), P(), P(), P(), P(), P(), P())
    return jax.shard_map(
        shards, mesh=mesh, in_specs=placed, out_specs=P(None, None, "lat", "lon"), check_vma=False
    )
```

```python
import math

import jax
import jax.numpy as jnp
from jax import lax
from jax.sharding import PartitionSpec as P

STEPS = 2
BATCHES = 2
NB = 256


RATE = 0.4
DEPTHS = (1.0, 0.6, 0.35)
COUPLE = ((1.0, 0.5, 0.25), (0.5, 1.0, 0.5), (0.25, 0.5, 1.0))


def ring_pairs(size, step):
    return [(i, (i + step) % size) for i in range(size)]


def lon_edges(array):
    size = lax.axis_size("lon")
    up = [(i, (i + 1) % size) for i in range(size)]
    down = [((i + 1) % size, i) for i in range(size)]
    left = lax.ppermute(array[..., -1:], "lon", up)
    right = lax.ppermute(array[..., :1], "lon", down)
    return left, right


def lat_shift(array, step):
    size = lax.axis_size("lat")
    source = lax.axis_index("lat") - step
    moved = lax.ppermute(array, "lat", ring_pairs(size, step))
    return jnp.where((source >= 0) & (source < size), moved, 0.0)


def lat_edges(array):
    before = lat_shift(array[:, :, -1:, :], 1)
    after = lat_shift(array[:, :, :1, :], -1)
    return before, after


def zonal(values, left, right):
    following = jnp.concatenate([values[..., 1:], right], axis=3)
    preceding = jnp.concatenate([left, values[..., :-1]], axis=3)
    return 0.5 * (following - preceding)


def meridional(values, before, after):
    following = jnp.concatenate([values[:, :, 1:, :], after], axis=2)
    preceding = jnp.concatenate([before, values[:, :, :-1, :]], axis=2)
    return 0.5 * (following - preceding)


def couple(height):
    return jnp.stack(
        [
            COUPLE[k][0] * height[0] + COUPLE[k][1] * height[1] + COUPLE[k][2] * height[2]
            for k in range(3)
        ]
    )


def march_prediction(running_member_set, rotation_frequency):
    height = running_member_set[0:3]
    eastward_speed = running_member_set[3:6]
    merid_vel = running_member_set[6:9]
    depths = jnp.array(DEPTHS, jnp.float32)[:, None, None, None]
    u_left, u_right = lon_edges(eastward_speed)
    v_before, v_after = lat_edges(merid_vel)
    height = height - RATE * depths * (
        zonal(eastward_speed, u_left, u_right) + meridional(merid_vel, v_before, v_after)
    )
    pressure = couple(height)
    p_left, p_right = lon_edges(pressure)
    p_before, p_after = lat_edges(pressure)
    eastward_speed = (
        eastward_speed
        + RATE * rotation_frequency * merid_vel
        - RATE * zonal(pressure, p_left, p_right)
    )
    merid_vel = (
        merid_vel
        - RATE * rotation_frequency * eastward_speed
        - RATE * meridional(pressure, p_before, p_after)
    )
    return jnp.concatenate([height, eastward_speed, merid_vel])


def statistics(priors, values, errors, member_count):
    mean_obs = jnp.mean(priors, axis=1, keepdims=True)
    anomaly = priors - mean_obs
    variance = jnp.sum(anomaly * anomaly, axis=1, keepdims=True) / (member_count - 1)
    obs_err = errors[:, None]
    denominator = variance + obs_err
    shrink = 1.0 / (1.0 + jnp.sqrt(obs_err / denominator))
    gains = (values[:, None] - mean_obs - shrink * anomaly) / denominator
    return (gains, anomaly)


def localize(cell_lon, cell_lat, lon_obs, lat_obs, radius_obs, grid_lon):
    lon_gap = (cell_lon[None, :] - lon_obs[:, None]) % grid_lon
    lon_gap = jnp.minimum(lon_gap, grid_lon - lon_gap)
    lat_gap = cell_lat[None, :] - lat_obs[:, None]
    distance_sq = (lon_gap * lon_gap + lat_gap * lat_gap).astype(jnp.float32)
    radius_sq = (radius_obs * radius_obs).astype(jnp.float32)[:, None]
    return jnp.square(jnp.maximum(1.0 - distance_sq / radius_sq, 0.0))


def tile_origin(state):
    _, _, rows_tile, cols_tile = state.shape
    return lax.axis_index("lon") * cols_tile, lax.axis_index("lat") * rows_tile


def owner_table(state, lon_obs, lat_obs, kind_obs):
    fields_count, _, rows_tile, cols_tile = state.shape
    lon_base, lat_base = tile_origin(state)
    row_hit = jnp.arange(rows_tile, dtype=jnp.int32)[None, :] == (lat_obs - lat_base)[:, None]
    col_hit = jnp.arange(cols_tile, dtype=jnp.int32)[None, :] == (lon_obs - lon_base)[:, None]
    cell = (row_hit[:, :, None] & col_hit[:, None, :]).astype(jnp.float32)
    picked = jnp.einsum("jrc,fmrc->jfm", cell, state, precision=lax.Precision.HIGHEST)
    field_hit = jnp.arange(fields_count, dtype=jnp.int32)[None, :] == kind_obs[:, None]
    return jnp.sum(jnp.where(field_hit[:, :, None], picked, 0.0), axis=1)


def update(state, gains, anomaly, weights):
    return jnp.concatenate(
        [update_group(state[f : f + 3], gains, anomaly, weights) for f in range(0, state.shape[0], 3)]
    )


def update_group(state, gains, anomaly, weights):
    fields_count, member_count, rows_tile, cols_tile = state.shape
    flattened = state.reshape(fields_count, member_count, rows_tile * cols_tile)
    deviation = flattened - jnp.mean(flattened, axis=1, keepdims=True)
    covariance = jnp.einsum(
        "om,fmc->foc", anomaly, deviation, precision=lax.Precision.HIGH
    ) / (member_count - 1)
    increment = jnp.einsum(
        "om,foc->fmc", gains, covariance * weights[None], precision=lax.Precision.HIGH
    )
    return (flattened + increment).reshape(state.shape)


def tile_weights(state, lon_obs, lat_obs, radius_obs):
    _, _, rows_tile, cols_tile = state.shape
    lon_base, lat_base = tile_origin(state)
    grid_lon = cols_tile * lax.axis_size("lon")
    cell_lat = lat_base + jnp.repeat(jnp.arange(rows_tile, dtype=jnp.int32), cols_tile)
    cell_lon = lon_base + jnp.tile(jnp.arange(cols_tile, dtype=jnp.int32), rows_tile)
    return localize(cell_lon, cell_lat, lon_obs, lat_obs, radius_obs, grid_lon)


def shards(
    ensemble, obs_lon, obs_lat, observation_field, obs_radius, batch_order, obs_value, obs_error
):
    fields_count, member_count, rows_tile, cols_tile = ensemble.shape
    lat_index = lax.axis_index("lat")
    lat_count = lax.axis_size("lat")
    lon_size = lax.axis_size("lon")
    lat_size = lax.axis_size("lat")
    grid_lon = cols_tile * lon_size
    mesh_northing = rows_tile * lat_count
    row_global = (lat_index * rows_tile + jnp.arange(rows_tile, dtype=jnp.int32)).astype(
        jnp.float32
    )
    rotation_frequency = (2.0 * jnp.sin(math.pi * ((row_global + 0.5) / mesh_northing - 0.5)))[
        :, None
    ]
    ints = jnp.stack([obs_lon, obs_lat, observation_field, obs_radius])[:, batch_order]
    floats = jnp.stack([obs_value, obs_error])[:, batch_order]
    batches = [
        (ints[:, b * NB : (b + 1) * NB], floats[:, b * NB : (b + 1) * NB]) for b in range(BATCHES)
    ]
    state = ensemble
    for step_index in range(STEPS):
        state = march_prediction(state, rotation_frequency)

    (lon0, lat0, kind0, radius0), (value0, error0) = batches[0]
    (lon1, lat1, kind1, radius1), (value1, error1) = batches[1]
    table0, table1 = jnp.split(owner_table(state, ints[0], ints[1], ints[2]), 2)
    both = jnp.concatenate([table0, table1])
    both = (
        both
        + lax.ppermute(both, "lon", ring_pairs(lon_size, 1))
        + lax.ppermute(both, "lon", ring_pairs(lon_size, -1))
    )
    wide0 = (
        both[:NB]
        + lax.ppermute(table0, "lon", ring_pairs(lon_size, 2))
        + lax.ppermute(table0, "lon", ring_pairs(lon_size, -2))
    )
    both = jnp.concatenate([wide0, both[NB:]])
    both = (
        both
        + lat_shift(both, 1)
        + lat_shift(both, -1)
    )
    priors = (
        both[:NB]
        + lat_shift(wide0, 2)
        + lat_shift(wide0, -2)
    )
    raw1 = both[NB:]
    gains, anomaly = statistics(priors, value0, error0, member_count)
    deviation = raw1 - jnp.mean(raw1, axis=1, keepdims=True)
    covariance = jnp.einsum(
        "om,jm->oj", anomaly, deviation, precision=lax.Precision.HIGH
    ) / (member_count - 1)
    weights = localize(lon1, lat1, lon0, lat0, radius0, grid_lon)
    increment = jnp.einsum("om,oj->jm", gains, covariance * weights, precision=lax.Precision.HIGH)
    priors1 = raw1 + increment
    state = update(state, gains, anomaly, tile_weights(state, lon0, lat0, radius0))
    gains, anomaly = statistics(priors1, value1, error1, member_count)
    state = update(state, gains, anomaly, tile_weights(state, lon1, lat1, radius1))
    return state.astype(jnp.bfloat16)


def solution(mesh):
    placed = (P(None, None, "lat", "lon"), P(), P(), P(), P(), P(), P(), P())
    return jax.shard_map(
        shards, mesh=mesh, in_specs=placed, out_specs=P(None, None, "lat", "lon"), check_vma=False
    )
```

```python
import math

import jax
import jax.numpy as jnp
from jax import lax
from jax.sharding import PartitionSpec as P

STEPS = 2
BATCHES = 2
NB = 256


RATE = 0.4
DEPTHS = (1.0, 0.6, 0.35)
COUPLE = ((1.0, 0.5, 0.25), (0.5, 1.0, 0.5), (0.25, 0.5, 1.0))


def ring_pairs(size, step):
    return [(i, (i + step) % size) for i in range(size)]


def line_pairs(size, step):
    return [(i, i + step) for i in range(size) if 0 <= i + step < size]


def lon_edges(array):
    size = lax.axis_size("lon")
    up = [(i, (i + 1) % size) for i in range(size)]
    down = [((i + 1) % size, i) for i in range(size)]
    left = lax.ppermute(array[..., -1:], "lon", up)
    right = lax.ppermute(array[..., :1], "lon", down)
    return left, right


def lat_edges(array):
    size = lax.axis_size("lat")
    up = [(i, i + 1) for i in range(size - 1)]
    down = [(i + 1, i) for i in range(size - 1)]
    before = lax.ppermute(array[:, :, -1:, :], "lat", up)
    after = lax.ppermute(array[:, :, :1, :], "lat", down)
    return before, after


def zonal(values, left, right):
    following = jnp.concatenate([values[..., 1:], right], axis=3)
    preceding = jnp.concatenate([left, values[..., :-1]], axis=3)
    return 0.5 * (following - preceding)


def meridional(values, before, after):
    following = jnp.concatenate([values[:, :, 1:, :], after], axis=2)
    preceding = jnp.concatenate([before, values[:, :, :-1, :]], axis=2)
    return 0.5 * (following - preceding)


def couple(height):
    return jnp.stack(
        [
            COUPLE[k][0] * height[0] + COUPLE[k][1] * height[1] + COUPLE[k][2] * height[2]
            for k in range(3)
        ]
    )


def march_prediction(running_member_set, rotation_frequency):
    height = running_member_set[0:3]
    eastward_speed = running_member_set[3:6]
    merid_vel = running_member_set[6:9]
    depths = jnp.array(DEPTHS, jnp.float32)[:, None, None, None]
    v_before, v_after = lat_edges(merid_vel)
    height = height - RATE * depths * (
        zonal_inside(eastward_speed) + meridional(merid_vel, v_before, v_after)
    )
    pressure = couple(height)
    p_before, p_after = lat_edges(pressure)
    eastward_speed = (
        eastward_speed + RATE * rotation_frequency * merid_vel - RATE * zonal_inside(pressure)
    )
    merid_vel = (
        merid_vel
        - RATE * rotation_frequency * eastward_speed
        - RATE * meridional(pressure, p_before, p_after)
    )
    return jnp.concatenate([height, eastward_speed, merid_vel])


def zonal_inside(values):
    return zonal(values, values[..., :1], values[..., -1:])


def lon_widened(state, width):
    size = lax.axis_size("lon")
    left = lax.ppermute(state[..., -width:], "lon", ring_pairs(size, 1))
    right = lax.ppermute(state[..., :width], "lon", ring_pairs(size, -1))
    return jnp.concatenate([left, state, right], axis=3)


def statistics(priors, values, errors, member_count):
    mean_obs = jnp.mean(priors, axis=1, keepdims=True)
    anomaly = priors - mean_obs
    variance = jnp.sum(anomaly * anomaly, axis=1, keepdims=True) / (member_count - 1)
    obs_err = errors[:, None]
    denominator = variance + obs_err
    shrink = 1.0 / (1.0 + jnp.sqrt(obs_err / denominator))
    gains = (values[:, None] - mean_obs - shrink * anomaly) / denominator
    return (gains, anomaly)


def localize(cell_lon, cell_lat, lon_obs, lat_obs, radius_obs, grid_lon):
    lon_gap = (cell_lon[None, :] - lon_obs[:, None]) % grid_lon
    lon_gap = jnp.minimum(lon_gap, grid_lon - lon_gap)
    lat_gap = cell_lat[None, :] - lat_obs[:, None]
    distance_sq = (lon_gap * lon_gap + lat_gap * lat_gap).astype(jnp.float32)
    radius_sq = (radius_obs * radius_obs).astype(jnp.float32)[:, None]
    return jnp.square(jnp.maximum(1.0 - distance_sq / radius_sq, 0.0))


def neighbourhood_sum(table):
    lon_n = lax.axis_size("lon")
    lat_n = lax.axis_size("lat")
    row = (
        table
        + lax.ppermute(table, "lon", ring_pairs(lon_n, 1))
        + lax.ppermute(table, "lon", ring_pairs(lon_n, -1))
    )
    return (
        row
        + lax.ppermute(row, "lat", line_pairs(lat_n, 1))
        + lax.ppermute(row, "lat", line_pairs(lat_n, -1))
    )


def tile_origin(state):
    _, _, rows_tile, cols_tile = state.shape
    return lax.axis_index("lon") * cols_tile, lax.axis_index("lat") * rows_tile


def owner_table(state, lon_obs, lat_obs, kind_obs):
    fields_count, _, rows_tile, cols_tile = state.shape
    lon_base, lat_base = tile_origin(state)
    row_hit = jnp.arange(rows_tile, dtype=jnp.int32)[None, :] == (lat_obs - lat_base)[:, None]
    col_hit = jnp.arange(cols_tile, dtype=jnp.int32)[None, :] == (lon_obs - lon_base)[:, None]
    cell = (row_hit[:, :, None] & col_hit[:, None, :]).astype(jnp.float32)
    picked = jnp.einsum("jrc,fmrc->jfm", cell, state, precision=lax.Precision.HIGHEST)
    field_hit = jnp.arange(fields_count, dtype=jnp.int32)[None, :] == kind_obs[:, None]
    return jnp.sum(jnp.where(field_hit[:, :, None], picked, 0.0), axis=1)


def update(state, gains, anomaly, weights):
    return jnp.concatenate(
        [update_group(state[f : f + 3], gains, anomaly, weights) for f in range(0, state.shape[0], 3)]
    )


def update_group(state, gains, anomaly, weights):
    fields_count, member_count, rows_tile, cols_tile = state.shape
    flattened = state.reshape(fields_count, member_count, rows_tile * cols_tile)
    deviation = flattened - jnp.mean(flattened, axis=1, keepdims=True)
    covariance = jnp.einsum(
        "om,fmc->foc", anomaly, deviation, precision=lax.Precision.HIGH
    ) / (member_count - 1)
    increment = jnp.einsum(
        "om,foc->fmc", gains, covariance * weights[None], precision=lax.Precision.HIGH
    )
    return (flattened + increment).reshape(state.shape)


def tile_weights(state, lon_obs, lat_obs, radius_obs):
    _, _, rows_tile, cols_tile = state.shape
    lon_base, lat_base = tile_origin(state)
    grid_lon = cols_tile * lax.axis_size("lon")
    cell_lat = lat_base + jnp.repeat(jnp.arange(rows_tile, dtype=jnp.int32), cols_tile)
    cell_lon = lon_base + jnp.tile(jnp.arange(cols_tile, dtype=jnp.int32), rows_tile)
    return localize(cell_lon, cell_lat, lon_obs, lat_obs, radius_obs, grid_lon)


def shards(
    ensemble, obs_lon, obs_lat, observation_field, obs_radius, batch_order, obs_value, obs_error
):
    fields_count, member_count, rows_tile, cols_tile = ensemble.shape
    lat_index = lax.axis_index("lat")
    lat_count = lax.axis_size("lat")
    lon_size = lax.axis_size("lon")
    lat_size = lax.axis_size("lat")
    grid_lon = cols_tile * lon_size
    mesh_northing = rows_tile * lat_count
    row_global = (lat_index * rows_tile + jnp.arange(rows_tile, dtype=jnp.int32)).astype(
        jnp.float32
    )
    rotation_frequency = (2.0 * jnp.sin(math.pi * ((row_global + 0.5) / mesh_northing - 0.5)))[
        :, None
    ]
    ints = jnp.stack([obs_lon, obs_lat, observation_field, obs_radius])[:, batch_order]
    floats = jnp.stack([obs_value, obs_error])[:, batch_order]
    batches = [
        (ints[:, b * NB : (b + 1) * NB], floats[:, b * NB : (b + 1) * NB]) for b in range(BATCHES)
    ]
    width = 2 * STEPS
    state = lon_widened(ensemble, width)
    for step_index in range(STEPS):
        state = march_prediction(state, rotation_frequency)
    state = state[..., width : width + cols_tile]

    (lon0, lat0, kind0, radius0), (value0, error0) = batches[0]
    (lon1, lat1, kind1, radius1), (value1, error1) = batches[1]
    table0, table1 = jnp.split(owner_table(state, ints[0], ints[1], ints[2]), 2)
    both = jnp.concatenate([table0, table1])
    both = (
        both
        + lax.ppermute(both, "lon", ring_pairs(lon_size, 1))
        + lax.ppermute(both, "lon", ring_pairs(lon_size, -1))
    )
    wide0 = (
        both[:NB]
        + lax.ppermute(table0, "lon", ring_pairs(lon_size, 2))
        + lax.ppermute(table0, "lon", ring_pairs(lon_size, -2))
    )
    both = jnp.concatenate([wide0, both[NB:]])
    both = (
        both
        + lax.ppermute(both, "lat", line_pairs(lat_size, 1))
        + lax.ppermute(both, "lat", line_pairs(lat_size, -1))
    )
    priors = (
        both[:NB]
        + lax.ppermute(wide0, "lat", line_pairs(lat_size, 2))
        + lax.ppermute(wide0, "lat", line_pairs(lat_size, -2))
    )
    raw1 = both[NB:]
    gains, anomaly = statistics(priors, value0, error0, member_count)
    deviation = raw1 - jnp.mean(raw1, axis=1, keepdims=True)
    covariance = jnp.einsum(
        "om,jm->oj", anomaly, deviation, precision=lax.Precision.HIGH
    ) / (member_count - 1)
    weights = localize(lon1, lat1, lon0, lat0, radius0, grid_lon)
    increment = jnp.einsum("om,oj->jm", gains, covariance * weights, precision=lax.Precision.HIGH)
    priors1 = raw1 + increment
    state = update(state, gains, anomaly, tile_weights(state, lon0, lat0, radius0))
    gains, anomaly = statistics(priors1, value1, error1, member_count)
    state = update(state, gains, anomaly, tile_weights(state, lon1, lat1, radius1))
    return state.astype(jnp.bfloat16)


def solution(mesh):
    placed = (P(None, None, "lat", "lon"), P(), P(), P(), P(), P(), P(), P())
    return jax.shard_map(
        shards, mesh=mesh, in_specs=placed, out_specs=P(None, None, "lat", "lon"), check_vma=False
    )
```

```python
import math

import jax
import jax.numpy as jnp
from jax import lax
from jax.sharding import PartitionSpec as P

STEPS = 2
BATCHES = 2
NB = 256


RATE = 0.4
DEPTHS = (1.0, 0.6, 0.35)
COUPLE = ((1.0, 0.5, 0.25), (0.5, 1.0, 0.5), (0.25, 0.5, 1.0))


def ring_pairs(size, step):
    return [(i, (i + step) % size) for i in range(size)]


def line_pairs(size, step):
    return [(i, i + step) for i in range(size) if 0 <= i + step < size]


def lon_edges(array):
    size = lax.axis_size("lon")
    up = [(i, (i + 1) % size) for i in range(size)]
    down = [((i + 1) % size, i) for i in range(size)]
    left = lax.ppermute(array[..., -1:], "lon", up)
    right = lax.ppermute(array[..., :1], "lon", down)
    return left, right


def lat_edges(array):
    size = lax.axis_size("lat")
    up = [(i, i + 1) for i in range(size - 1)]
    down = [(i + 1, i) for i in range(size - 1)]
    before = lax.ppermute(array[:, :, -1:, :], "lat", up)
    after = lax.ppermute(array[:, :, :1, :], "lat", down)
    return before, after


def zonal(values, left, right):
    following = jnp.concatenate([values[..., 1:], right], axis=3)
    preceding = jnp.concatenate([left, values[..., :-1]], axis=3)
    return 0.5 * (following - preceding)


def meridional(values, before, after):
    following = jnp.concatenate([values[:, :, 1:, :], after], axis=2)
    preceding = jnp.concatenate([before, values[:, :, :-1, :]], axis=2)
    return 0.5 * (following - preceding)


def couple(height):
    return jnp.stack(
        [
            COUPLE[k][0] * height[0] + COUPLE[k][1] * height[1] + COUPLE[k][2] * height[2]
            for k in range(3)
        ]
    )


def march_prediction(running_member_set, rotation_frequency):
    height = running_member_set[0:3]
    eastward_speed = running_member_set[3:6]
    merid_vel = running_member_set[6:9]
    depths = jnp.array(DEPTHS, jnp.float32)[:, None, None, None]
    v_before, v_after = lat_edges(merid_vel)
    height = height - RATE * depths * (
        zonal_inside(eastward_speed) + meridional(merid_vel, v_before, v_after)
    )
    pressure = couple(height)
    p_before, p_after = lat_edges(pressure)
    eastward_speed = (
        eastward_speed + RATE * rotation_frequency * merid_vel - RATE * zonal_inside(pressure)
    )
    merid_vel = (
        merid_vel
        - RATE * rotation_frequency * eastward_speed
        - RATE * meridional(pressure, p_before, p_after)
    )
    return jnp.concatenate([height, eastward_speed, merid_vel])


def zonal_inside(values):
    return zonal(values, values[..., :1], values[..., -1:])


def lon_widened(state, width):
    size = lax.axis_size("lon")
    left = lax.ppermute(state[..., -width:], "lon", ring_pairs(size, 1))
    right = lax.ppermute(state[..., :width], "lon", ring_pairs(size, -1))
    return jnp.concatenate([left, state, right], axis=3)


def statistics(priors, values, errors, member_count):
    mean_obs = jnp.mean(priors, axis=1, keepdims=True)
    anomaly = priors - mean_obs
    variance = jnp.sum(anomaly * anomaly, axis=1, keepdims=True) / (member_count - 1)
    obs_err = errors[:, None]
    denominator = variance + obs_err
    shrink = 1.0 / (1.0 + jnp.sqrt(obs_err / denominator))
    gains = (values[:, None] - mean_obs - shrink * anomaly) / denominator
    return (gains, anomaly)


def localize(cell_lon, cell_lat, lon_obs, lat_obs, radius_obs, grid_lon):
    lon_gap = (cell_lon[None, :] - lon_obs[:, None]) % grid_lon
    lon_gap = jnp.minimum(lon_gap, grid_lon - lon_gap)
    lat_gap = cell_lat[None, :] - lat_obs[:, None]
    distance_sq = (lon_gap * lon_gap + lat_gap * lat_gap).astype(jnp.float32)
    radius_sq = (radius_obs * radius_obs).astype(jnp.float32)[:, None]
    return jnp.square(jnp.maximum(1.0 - distance_sq / radius_sq, 0.0))


def neighbourhood_sum(table):
    lon_n = lax.axis_size("lon")
    lat_n = lax.axis_size("lat")
    row = (
        table
        + lax.ppermute(table, "lon", ring_pairs(lon_n, 1))
        + lax.ppermute(table, "lon", ring_pairs(lon_n, -1))
    )
    return (
        row
        + lax.ppermute(row, "lat", line_pairs(lat_n, 1))
        + lax.ppermute(row, "lat", line_pairs(lat_n, -1))
    )


def tile_origin(state):
    _, _, rows_tile, cols_tile = state.shape
    return lax.axis_index("lon") * cols_tile, lax.axis_index("lat") * rows_tile


def owner_table(state, lon_obs, lat_obs, kind_obs):
    fields_count, _, rows_tile, cols_tile = state.shape
    lon_base, lat_base = tile_origin(state)
    row_hit = jnp.arange(rows_tile, dtype=jnp.int32)[None, :] == (lat_obs - lat_base)[:, None]
    col_hit = jnp.arange(cols_tile, dtype=jnp.int32)[None, :] == (lon_obs - lon_base)[:, None]
    cell = (row_hit[:, :, None] & col_hit[:, None, :]).astype(jnp.float32)
    picked = jnp.einsum("jrc,fmrc->jfm", cell, state, precision=lax.Precision.HIGHEST)
    field_hit = jnp.arange(fields_count, dtype=jnp.int32)[None, :] == kind_obs[:, None]
    return jnp.sum(jnp.where(field_hit[:, :, None], picked, 0.0), axis=1)


TILE_SLOTS = 32
WINDOW_SLOTS = 64


def slots(tile_lat, tile_lon, lat_at, lon_at, reach, count):
    lon_n = lax.axis_size("lon")
    gap = (tile_lon - lon_at) % lon_n
    member = (tile_lat == lat_at) & ((gap <= reach) | (gap >= lon_n - reach))
    rank = jnp.cumsum(member.astype(jnp.int32)) - 1
    hit = member[None, :] & (rank[None, :] == jnp.arange(count, dtype=jnp.int32)[:, None])
    return hit.astype(jnp.float32)


def pack(selection, table):
    return jnp.einsum("ko,om->km", selection, table, precision=lax.Precision.HIGHEST)


def unpack(selection, packed):
    return jnp.einsum("ko,km->om", selection, packed, precision=lax.Precision.HIGHEST)


def packed_exchange(tables, tile_lat, tile_lon):
    lon_n = lax.axis_size("lon")
    lat_i = lax.axis_index("lat")
    lon_j = lax.axis_index("lon")
    own = pack(slots(tile_lat, tile_lon, lat_i, lon_j, 0, TILE_SLOTS), tables)
    row = tables
    for step in (1, -1, 2, -2):
        moved = lax.ppermute(own, "lon", ring_pairs(lon_n, step))
        row = row + unpack(slots(tile_lat, tile_lon, lat_i, lon_j - step, 0, TILE_SLOTS), moved)
    sent = pack(slots(tile_lat, tile_lon, lat_i, lon_j, 2, WINDOW_SLOTS), row)
    total = row
    for step in (1, -1, 2, -2):
        moved = lat_shift(sent, step)
        total = total + unpack(
            slots(tile_lat, tile_lon, lat_i - step, lon_j, 2, WINDOW_SLOTS), moved
        )
    return total


def full_exchange(tables, lon_size):
    table0 = tables[:NB]
    both = (
        tables
        + lax.ppermute(tables, "lon", ring_pairs(lon_size, 1))
        + lax.ppermute(tables, "lon", ring_pairs(lon_size, -1))
    )
    wide0 = (
        both[:NB]
        + lax.ppermute(table0, "lon", ring_pairs(lon_size, 2))
        + lax.ppermute(table0, "lon", ring_pairs(lon_size, -2))
    )
    both = jnp.concatenate([wide0, both[NB:]])
    both = both + lat_shift(both, 1) + lat_shift(both, -1)
    return jnp.concatenate(
        [both[:NB] + lat_shift(wide0, 2) + lat_shift(wide0, -2), both[NB:]]
    )


def lat_shift(array, step):
    size = lax.axis_size("lat")
    pairs = [(i, i + step) for i in range(size) if 0 <= i + step < size]
    return lax.ppermute(array, "lat", pairs)


def update(state, gains, anomaly, weights):
    return jnp.concatenate(
        [update_group(state[f : f + 3], gains, anomaly, weights) for f in range(0, state.shape[0], 3)]
    )


def update_group(state, gains, anomaly, weights):
    fields_count, member_count, rows_tile, cols_tile = state.shape
    flattened = state.reshape(fields_count, member_count, rows_tile * cols_tile)
    deviation = flattened - jnp.mean(flattened, axis=1, keepdims=True)
    covariance = jnp.einsum(
        "om,fmc->foc", anomaly, deviation, precision=lax.Precision.HIGH
    ) / (member_count - 1)
    increment = jnp.einsum(
        "om,foc->fmc", gains, covariance * weights[None], precision=lax.Precision.HIGH
    )
    return (flattened + increment).reshape(state.shape)


def tile_weights(state, lon_obs, lat_obs, radius_obs):
    _, _, rows_tile, cols_tile = state.shape
    lon_base, lat_base = tile_origin(state)
    grid_lon = cols_tile * lax.axis_size("lon")
    cell_lat = lat_base + jnp.repeat(jnp.arange(rows_tile, dtype=jnp.int32), cols_tile)
    cell_lon = lon_base + jnp.tile(jnp.arange(cols_tile, dtype=jnp.int32), rows_tile)
    return localize(cell_lon, cell_lat, lon_obs, lat_obs, radius_obs, grid_lon)


def shards(
    ensemble, obs_lon, obs_lat, observation_field, obs_radius, batch_order, obs_value, obs_error
):
    fields_count, member_count, rows_tile, cols_tile = ensemble.shape
    lat_index = lax.axis_index("lat")
    lat_count = lax.axis_size("lat")
    lon_size = lax.axis_size("lon")
    lat_size = lax.axis_size("lat")
    grid_lon = cols_tile * lon_size
    mesh_northing = rows_tile * lat_count
    row_global = (lat_index * rows_tile + jnp.arange(rows_tile, dtype=jnp.int32)).astype(
        jnp.float32
    )
    rotation_frequency = (2.0 * jnp.sin(math.pi * ((row_global + 0.5) / mesh_northing - 0.5)))[
        :, None
    ]
    ints = jnp.stack([obs_lon, obs_lat, observation_field, obs_radius])[:, batch_order]
    floats = jnp.stack([obs_value, obs_error])[:, batch_order]
    batches = [
        (ints[:, b * NB : (b + 1) * NB], floats[:, b * NB : (b + 1) * NB]) for b in range(BATCHES)
    ]
    width = 2 * STEPS
    state = lon_widened(ensemble, width)
    for step_index in range(STEPS):
        state = march_prediction(state, rotation_frequency)
    state = state[..., width : width + cols_tile]

    (lon0, lat0, kind0, radius0), (value0, error0) = batches[0]
    (lon1, lat1, kind1, radius1), (value1, error1) = batches[1]
    table0, table1 = jnp.split(owner_table(state, ints[0], ints[1], ints[2]), 2)
    tile_lat = ints[1] // rows_tile
    tile_lon = ints[0] // cols_tile
    per_tile = jnp.sum(
        (tile_lat * lon_size + tile_lon)[:, None]
        == jnp.arange(lat_size * lon_size, dtype=jnp.int32)[None, :],
        axis=0,
    ).reshape(lat_size, lon_size)
    per_window = sum(jnp.roll(per_tile, d, axis=1) for d in range(-2, 3))
    packable = (jnp.max(per_tile) <= TILE_SLOTS) & (jnp.max(per_window) <= WINDOW_SLOTS)
    tables = jnp.concatenate([table0, table1])
    both = lax.cond(
        packable,
        lambda t: packed_exchange(t, tile_lat, tile_lon),
        lambda t: full_exchange(t, lon_size),
        tables,
    )
    priors = both[:NB]
    raw1 = both[NB:]
    gains, anomaly = statistics(priors, value0, error0, member_count)
    deviation = raw1 - jnp.mean(raw1, axis=1, keepdims=True)
    covariance = jnp.einsum(
        "om,jm->oj", anomaly, deviation, precision=lax.Precision.HIGH
    ) / (member_count - 1)
    weights = localize(lon1, lat1, lon0, lat0, radius0, grid_lon)
    increment = jnp.einsum("om,oj->jm", gains, covariance * weights, precision=lax.Precision.HIGH)
    priors1 = raw1 + increment
    state = update(state, gains, anomaly, tile_weights(state, lon0, lat0, radius0))
    gains, anomaly = statistics(priors1, value1, error1, member_count)
    state = update(state, gains, anomaly, tile_weights(state, lon1, lat1, radius1))
    return state.astype(jnp.bfloat16)


def solution(mesh):
    placed = (P(None, None, "lat", "lon"), P(), P(), P(), P(), P(), P(), P())
    return jax.shard_map(
        shards, mesh=mesh, in_specs=placed, out_specs=P(None, None, "lat", "lon"), check_vma=False
    )
```

```python
import math

import jax
import jax.numpy as jnp
from jax import lax
from jax.sharding import PartitionSpec as P

STEPS = 2
BATCHES = 2
NB = 256


RATE = 0.4
DEPTHS = (1.0, 0.6, 0.35)
COUPLE = ((1.0, 0.5, 0.25), (0.5, 1.0, 0.5), (0.25, 0.5, 1.0))


def ring_pairs(size, step):
    return [(i, (i + step) % size) for i in range(size)]


def line_pairs(size, step):
    return [(i, i + step) for i in range(size) if 0 <= i + step < size]


def lon_edges(array):
    size = lax.axis_size("lon")
    up = [(i, (i + 1) % size) for i in range(size)]
    down = [((i + 1) % size, i) for i in range(size)]
    left = lax.ppermute(array[..., -1:], "lon", up)
    right = lax.ppermute(array[..., :1], "lon", down)
    return left, right


def lat_edges(array):
    size = lax.axis_size("lat")
    up = [(i, i + 1) for i in range(size - 1)]
    down = [(i + 1, i) for i in range(size - 1)]
    before = lax.ppermute(array[:, :, -1:, :], "lat", up)
    after = lax.ppermute(array[:, :, :1, :], "lat", down)
    return before, after


def zonal(values, left, right):
    following = jnp.concatenate([values[..., 1:], right], axis=3)
    preceding = jnp.concatenate([left, values[..., :-1]], axis=3)
    return 0.5 * (following - preceding)


def meridional(values, before, after):
    following = jnp.concatenate([values[:, :, 1:, :], after], axis=2)
    preceding = jnp.concatenate([before, values[:, :, :-1, :]], axis=2)
    return 0.5 * (following - preceding)


def couple(height):
    return jnp.stack(
        [
            COUPLE[k][0] * height[0] + COUPLE[k][1] * height[1] + COUPLE[k][2] * height[2]
            for k in range(3)
        ]
    )


def march_prediction(running_member_set, rotation_frequency):
    height = running_member_set[0:3]
    eastward_speed = running_member_set[3:6]
    merid_vel = running_member_set[6:9]
    depths = jnp.array(DEPTHS, jnp.float32)[:, None, None, None]
    v_before, v_after = lat_edges(merid_vel)
    height = height - RATE * depths * (
        zonal_inside(eastward_speed) + meridional(merid_vel, v_before, v_after)
    )
    pressure = couple(height)
    p_before, p_after = lat_edges(pressure)
    eastward_speed = (
        eastward_speed + RATE * rotation_frequency * merid_vel - RATE * zonal_inside(pressure)
    )
    merid_vel = (
        merid_vel
        - RATE * rotation_frequency * eastward_speed
        - RATE * meridional(pressure, p_before, p_after)
    )
    return jnp.concatenate([height, eastward_speed, merid_vel])


def zonal_inside(values):
    return zonal(values, values[..., :1], values[..., -1:])


def lon_widened(state, width):
    size = lax.axis_size("lon")
    left = lax.ppermute(state[..., -width:], "lon", ring_pairs(size, 1))
    right = lax.ppermute(state[..., :width], "lon", ring_pairs(size, -1))
    return jnp.concatenate([left, state, right], axis=3)


def statistics(priors, values, errors, member_count):
    mean_obs = jnp.mean(priors, axis=1, keepdims=True)
    anomaly = priors - mean_obs
    variance = jnp.sum(anomaly * anomaly, axis=1, keepdims=True) / (member_count - 1)
    obs_err = errors[:, None]
    denominator = variance + obs_err
    shrink = 1.0 / (1.0 + jnp.sqrt(obs_err / denominator))
    gains = (values[:, None] - mean_obs - shrink * anomaly) / denominator
    return (gains, anomaly)


def localize(cell_lon, cell_lat, lon_obs, lat_obs, radius_obs, grid_lon):
    lon_gap = (cell_lon[None, :] - lon_obs[:, None]) % grid_lon
    lon_gap = jnp.minimum(lon_gap, grid_lon - lon_gap)
    lat_gap = cell_lat[None, :] - lat_obs[:, None]
    distance_sq = (lon_gap * lon_gap + lat_gap * lat_gap).astype(jnp.float32)
    radius_sq = (radius_obs * radius_obs).astype(jnp.float32)[:, None]
    return jnp.square(jnp.maximum(1.0 - distance_sq / radius_sq, 0.0))


def neighbourhood_sum(table):
    lon_n = lax.axis_size("lon")
    lat_n = lax.axis_size("lat")
    row = (
        table
        + lax.ppermute(table, "lon", ring_pairs(lon_n, 1))
        + lax.ppermute(table, "lon", ring_pairs(lon_n, -1))
    )
    return (
        row
        + lax.ppermute(row, "lat", line_pairs(lat_n, 1))
        + lax.ppermute(row, "lat", line_pairs(lat_n, -1))
    )


def tile_origin(state):
    _, _, rows_tile, cols_tile = state.shape
    return lax.axis_index("lon") * cols_tile, lax.axis_index("lat") * rows_tile


REACH = BATCHES * (8 - 1)


def lat_shift(array, step):
    size = lax.axis_size("lat")
    pairs = [(i, i + step) for i in range(size) if 0 <= i + step < size]
    return lax.ppermute(array, "lat", pairs)


def band_table(wide, lon_obs, lat_obs, kind_obs, width):
    fields_count, _, rows_tile, wide_cols = wide.shape
    cols_tile = wide_cols - 2 * width
    grid_lon = cols_tile * lax.axis_size("lon")
    lon_base = lax.axis_index("lon") * cols_tile
    lat_base = lax.axis_index("lat") * rows_tile
    column = (lon_obs - lon_base + width) % grid_lon
    inside = (column >= width - REACH) & (column < width + cols_tile + REACH)
    row_hit = jnp.arange(rows_tile, dtype=jnp.int32)[None, :] == (lat_obs - lat_base)[:, None]
    col_hit = (jnp.arange(wide_cols, dtype=jnp.int32)[None, :] == column[:, None]) & inside[:, None]
    cell = (row_hit[:, :, None] & col_hit[:, None, :]).astype(jnp.float32)
    picked = jnp.einsum("jrc,fmrc->jfm", cell, wide, precision=lax.Precision.HIGHEST)
    field_hit = jnp.arange(fields_count, dtype=jnp.int32)[None, :] == kind_obs[:, None]
    return jnp.sum(jnp.where(field_hit[:, :, None], picked, 0.0), axis=1)


def owner_table(state, lon_obs, lat_obs, kind_obs):
    fields_count, _, rows_tile, cols_tile = state.shape
    lon_base, lat_base = tile_origin(state)
    row_hit = jnp.arange(rows_tile, dtype=jnp.int32)[None, :] == (lat_obs - lat_base)[:, None]
    col_hit = jnp.arange(cols_tile, dtype=jnp.int32)[None, :] == (lon_obs - lon_base)[:, None]
    cell = (row_hit[:, :, None] & col_hit[:, None, :]).astype(jnp.float32)
    picked = jnp.einsum("jrc,fmrc->jfm", cell, state, precision=lax.Precision.HIGHEST)
    field_hit = jnp.arange(fields_count, dtype=jnp.int32)[None, :] == kind_obs[:, None]
    return jnp.sum(jnp.where(field_hit[:, :, None], picked, 0.0), axis=1)


def update(state, gains, anomaly, weights):
    return jnp.concatenate(
        [update_group(state[f : f + 3], gains, anomaly, weights) for f in range(0, state.shape[0], 3)]
    )


def update_group(state, gains, anomaly, weights):
    fields_count, member_count, rows_tile, cols_tile = state.shape
    flattened = state.reshape(fields_count, member_count, rows_tile * cols_tile)
    deviation = flattened - jnp.mean(flattened, axis=1, keepdims=True)
    covariance = jnp.einsum(
        "om,fmc->foc", anomaly, deviation, precision=lax.Precision.HIGH
    ) / (member_count - 1)
    increment = jnp.einsum(
        "om,foc->fmc", gains, covariance * weights[None], precision=lax.Precision.HIGH
    )
    return (flattened + increment).reshape(state.shape)


def tile_weights(state, lon_obs, lat_obs, radius_obs):
    _, _, rows_tile, cols_tile = state.shape
    lon_base, lat_base = tile_origin(state)
    grid_lon = cols_tile * lax.axis_size("lon")
    cell_lat = lat_base + jnp.repeat(jnp.arange(rows_tile, dtype=jnp.int32), cols_tile)
    cell_lon = lon_base + jnp.tile(jnp.arange(cols_tile, dtype=jnp.int32), rows_tile)
    return localize(cell_lon, cell_lat, lon_obs, lat_obs, radius_obs, grid_lon)


def shards(
    ensemble, obs_lon, obs_lat, observation_field, obs_radius, batch_order, obs_value, obs_error
):
    fields_count, member_count, rows_tile, cols_tile = ensemble.shape
    lat_index = lax.axis_index("lat")
    lat_count = lax.axis_size("lat")
    lon_size = lax.axis_size("lon")
    lat_size = lax.axis_size("lat")
    grid_lon = cols_tile * lon_size
    mesh_northing = rows_tile * lat_count
    row_global = (lat_index * rows_tile + jnp.arange(rows_tile, dtype=jnp.int32)).astype(
        jnp.float32
    )
    rotation_frequency = (2.0 * jnp.sin(math.pi * ((row_global + 0.5) / mesh_northing - 0.5)))[
        :, None
    ]
    ints = jnp.stack([obs_lon, obs_lat, observation_field, obs_radius])[:, batch_order]
    floats = jnp.stack([obs_value, obs_error])[:, batch_order]
    batches = [
        (ints[:, b * NB : (b + 1) * NB], floats[:, b * NB : (b + 1) * NB]) for b in range(BATCHES)
    ]
    width = 2 * STEPS + REACH
    state = lon_widened(ensemble, width)
    for step_index in range(STEPS):
        state = march_prediction(state, rotation_frequency)
    band = band_table(state, ints[0], ints[1], ints[2], width)
    state = state[..., width : width + cols_tile]

    (lon0, lat0, kind0, radius0), (value0, error0) = batches[0]
    (lon1, lat1, kind1, radius1), (value1, error1) = batches[1]
    table0 = band[:NB]
    both = band + lat_shift(band, 1) + lat_shift(band, -1)
    priors = both[:NB] + lat_shift(table0, 2) + lat_shift(table0, -2)
    raw1 = both[NB:]
    gains, anomaly = statistics(priors, value0, error0, member_count)
    deviation = raw1 - jnp.mean(raw1, axis=1, keepdims=True)
    covariance = jnp.einsum(
        "om,jm->oj", anomaly, deviation, precision=lax.Precision.HIGH
    ) / (member_count - 1)
    weights = localize(lon1, lat1, lon0, lat0, radius0, grid_lon)
    increment = jnp.einsum("om,oj->jm", gains, covariance * weights, precision=lax.Precision.HIGH)
    priors1 = raw1 + increment
    state = update(state, gains, anomaly, tile_weights(state, lon0, lat0, radius0))
    gains, anomaly = statistics(priors1, value1, error1, member_count)
    state = update(state, gains, anomaly, tile_weights(state, lon1, lat1, radius1))
    return state.astype(jnp.bfloat16)


def solution(mesh):
    placed = (P(None, None, "lat", "lon"), P(), P(), P(), P(), P(), P(), P())
    return jax.shard_map(
        shards, mesh=mesh, in_specs=placed, out_specs=P(None, None, "lat", "lon"), check_vma=False
    )
```

```python
import math

import jax
import jax.numpy as jnp
from jax import lax
from jax.sharding import PartitionSpec as P

STEPS = 2
BATCHES = 2
NB = 256


RATE = 0.4
DEPTHS = (1.0, 0.6, 0.35)
COUPLE = ((1.0, 0.5, 0.25), (0.5, 1.0, 0.5), (0.25, 0.5, 1.0))


def ring_pairs(size, step):
    return [(i, (i + step) % size) for i in range(size)]


def line_pairs(size, step):
    return [(i, i + step) for i in range(size) if 0 <= i + step < size]


def lon_edges(array):
    size = lax.axis_size("lon")
    up = [(i, (i + 1) % size) for i in range(size)]
    down = [((i + 1) % size, i) for i in range(size)]
    left = lax.ppermute(array[..., -1:], "lon", up)
    right = lax.ppermute(array[..., :1], "lon", down)
    return left, right


def lat_edges(array):
    size = lax.axis_size("lat")
    up = [(i, i + 1) for i in range(size - 1)]
    down = [(i + 1, i) for i in range(size - 1)]
    before = lax.ppermute(array[:, :, -1:, :], "lat", up)
    after = lax.ppermute(array[:, :, :1, :], "lat", down)
    return before, after


def zonal(values, left, right):
    following = jnp.concatenate([values[..., 1:], right], axis=3)
    preceding = jnp.concatenate([left, values[..., :-1]], axis=3)
    return 0.5 * (following - preceding)


def meridional(values, before, after):
    following = jnp.concatenate([values[:, :, 1:, :], after], axis=2)
    preceding = jnp.concatenate([before, values[:, :, :-1, :]], axis=2)
    return 0.5 * (following - preceding)


def couple(height):
    return jnp.stack(
        [
            COUPLE[k][0] * height[0] + COUPLE[k][1] * height[1] + COUPLE[k][2] * height[2]
            for k in range(3)
        ]
    )


def march_prediction(running_member_set, rotation_frequency):
    height = running_member_set[0:3]
    eastward_speed = running_member_set[3:6]
    merid_vel = running_member_set[6:9]
    depths = jnp.array(DEPTHS, jnp.float32)[:, None, None, None]
    v_before, v_after = lat_edges(merid_vel)
    height = height - RATE * depths * (
        zonal_inside(eastward_speed) + meridional(merid_vel, v_before, v_after)
    )
    pressure = couple(height)
    p_before, p_after = lat_edges(pressure)
    eastward_speed = (
        eastward_speed + RATE * rotation_frequency * merid_vel - RATE * zonal_inside(pressure)
    )
    merid_vel = (
        merid_vel
        - RATE * rotation_frequency * eastward_speed
        - RATE * meridional(pressure, p_before, p_after)
    )
    return jnp.concatenate([height, eastward_speed, merid_vel])


def zonal_inside(values):
    return zonal(values, values[..., :1], values[..., -1:])


def lon_widened(state, width):
    size = lax.axis_size("lon")
    left = lax.ppermute(state[..., -width:], "lon", ring_pairs(size, 1))
    right = lax.ppermute(state[..., :width], "lon", ring_pairs(size, -1))
    return jnp.concatenate([left, state, right], axis=3)


def statistics(priors, values, errors, member_count):
    mean_obs = jnp.mean(priors, axis=1, keepdims=True)
    anomaly = priors - mean_obs
    variance = jnp.sum(anomaly * anomaly, axis=1, keepdims=True) / (member_count - 1)
    obs_err = errors[:, None]
    denominator = variance + obs_err
    shrink = 1.0 / (1.0 + jnp.sqrt(obs_err / denominator))
    gains = (values[:, None] - mean_obs - shrink * anomaly) / denominator
    return (gains, anomaly)


def localize(cell_lon, cell_lat, lon_obs, lat_obs, radius_obs, grid_lon):
    lon_gap = (cell_lon[None, :] - lon_obs[:, None]) % grid_lon
    lon_gap = jnp.minimum(lon_gap, grid_lon - lon_gap)
    lat_gap = cell_lat[None, :] - lat_obs[:, None]
    distance_sq = (lon_gap * lon_gap + lat_gap * lat_gap).astype(jnp.float32)
    radius_sq = (radius_obs * radius_obs).astype(jnp.float32)[:, None]
    return jnp.square(jnp.maximum(1.0 - distance_sq / radius_sq, 0.0))


def neighbourhood_sum(table):
    lon_n = lax.axis_size("lon")
    lat_n = lax.axis_size("lat")
    row = (
        table
        + lax.ppermute(table, "lon", ring_pairs(lon_n, 1))
        + lax.ppermute(table, "lon", ring_pairs(lon_n, -1))
    )
    return (
        row
        + lax.ppermute(row, "lat", line_pairs(lat_n, 1))
        + lax.ppermute(row, "lat", line_pairs(lat_n, -1))
    )


def tile_origin(state):
    _, _, rows_tile, cols_tile = state.shape
    return lax.axis_index("lon") * cols_tile, lax.axis_index("lat") * rows_tile


REACH = BATCHES * (8 - 1)


def lat_shift(array, step):
    size = lax.axis_size("lat")
    pairs = [(i, i + step) for i in range(size) if 0 <= i + step < size]
    return lax.ppermute(array, "lat", pairs)


def band_table(wide, lon_obs, lat_obs, kind_obs, width):
    fields_count, _, rows_tile, wide_cols = wide.shape
    cols_tile = wide_cols - 2 * width
    grid_lon = cols_tile * lax.axis_size("lon")
    lon_base = lax.axis_index("lon") * cols_tile
    lat_base = lax.axis_index("lat") * rows_tile
    column = (lon_obs - lon_base + width) % grid_lon
    inside = (column >= width - REACH) & (column < width + cols_tile + REACH)
    row_hit = jnp.arange(rows_tile, dtype=jnp.int32)[None, :] == (lat_obs - lat_base)[:, None]
    col_hit = (jnp.arange(wide_cols, dtype=jnp.int32)[None, :] == column[:, None]) & inside[:, None]
    cell = (row_hit[:, :, None] & col_hit[:, None, :]).astype(jnp.float32)
    picked = jnp.einsum("jrc,fmrc->jfm", cell, wide, precision=lax.Precision.HIGHEST)
    field_hit = jnp.arange(fields_count, dtype=jnp.int32)[None, :] == kind_obs[:, None]
    return jnp.sum(jnp.where(field_hit[:, :, None], picked, 0.0), axis=1)


def owner_table(state, lon_obs, lat_obs, kind_obs):
    fields_count, _, rows_tile, cols_tile = state.shape
    lon_base, lat_base = tile_origin(state)
    row_hit = jnp.arange(rows_tile, dtype=jnp.int32)[None, :] == (lat_obs - lat_base)[:, None]
    col_hit = jnp.arange(cols_tile, dtype=jnp.int32)[None, :] == (lon_obs - lon_base)[:, None]
    cell = (row_hit[:, :, None] & col_hit[:, None, :]).astype(jnp.float32)
    picked = jnp.einsum("jrc,fmrc->jfm", cell, state, precision=lax.Precision.HIGHEST)
    field_hit = jnp.arange(fields_count, dtype=jnp.int32)[None, :] == kind_obs[:, None]
    return jnp.sum(jnp.where(field_hit[:, :, None], picked, 0.0), axis=1)


def update(state, gains, anomaly, weights):
    fields_count, member_count, rows_tile, cols_tile = state.shape
    flattened = state.reshape(fields_count, member_count, rows_tile * cols_tile)
    deviation = flattened - jnp.mean(flattened, axis=1, keepdims=True)
    covariance = jnp.einsum(
        "om,fmc->foc", anomaly, deviation, precision=lax.Precision.HIGH
    ) / (member_count - 1)
    increment = jnp.einsum(
        "om,foc->fmc", gains, covariance * weights[None], precision=lax.Precision.HIGH
    )
    return (flattened + increment).reshape(state.shape)


def tile_weights(state, lon_obs, lat_obs, radius_obs):
    _, _, rows_tile, cols_tile = state.shape
    lon_base, lat_base = tile_origin(state)
    grid_lon = cols_tile * lax.axis_size("lon")
    cell_lat = lat_base + jnp.repeat(jnp.arange(rows_tile, dtype=jnp.int32), cols_tile)
    cell_lon = lon_base + jnp.tile(jnp.arange(cols_tile, dtype=jnp.int32), rows_tile)
    return localize(cell_lon, cell_lat, lon_obs, lat_obs, radius_obs, grid_lon)


def shards(
    ensemble, obs_lon, obs_lat, observation_field, obs_radius, batch_order, obs_value, obs_error
):
    fields_count, member_count, rows_tile, cols_tile = ensemble.shape
    lat_index = lax.axis_index("lat")
    lat_count = lax.axis_size("lat")
    lon_size = lax.axis_size("lon")
    lat_size = lax.axis_size("lat")
    grid_lon = cols_tile * lon_size
    mesh_northing = rows_tile * lat_count
    row_global = (lat_index * rows_tile + jnp.arange(rows_tile, dtype=jnp.int32)).astype(
        jnp.float32
    )
    rotation_frequency = (2.0 * jnp.sin(math.pi * ((row_global + 0.5) / mesh_northing - 0.5)))[
        :, None
    ]
    ints = jnp.stack([obs_lon, obs_lat, observation_field, obs_radius])[:, batch_order]
    floats = jnp.stack([obs_value, obs_error])[:, batch_order]
    batches = [
        (ints[:, b * NB : (b + 1) * NB], floats[:, b * NB : (b + 1) * NB]) for b in range(BATCHES)
    ]
    width = 2 * STEPS + REACH
    state = lon_widened(ensemble, width)
    for step_index in range(STEPS):
        state = march_prediction(state, rotation_frequency)
    band = band_table(state, ints[0], ints[1], ints[2], width)
    state = state[..., width : width + cols_tile]

    (lon0, lat0, kind0, radius0), (value0, error0) = batches[0]
    (lon1, lat1, kind1, radius1), (value1, error1) = batches[1]
    table0 = band[:NB]
    both = band + lat_shift(band, 1) + lat_shift(band, -1)
    priors = both[:NB] + lat_shift(table0, 2) + lat_shift(table0, -2)
    raw1 = both[NB:]
    gains, anomaly = statistics(priors, value0, error0, member_count)
    deviation = raw1 - jnp.mean(raw1, axis=1, keepdims=True)
    covariance = jnp.einsum(
        "om,jm->oj", anomaly, deviation, precision=lax.Precision.HIGH
    ) / (member_count - 1)
    weights = localize(lon1, lat1, lon0, lat0, radius0, grid_lon)
    increment = jnp.einsum("om,oj->jm", gains, covariance * weights, precision=lax.Precision.HIGH)
    priors1 = raw1 + increment
    state = update(state, gains, anomaly, tile_weights(state, lon0, lat0, radius0))
    gains, anomaly = statistics(priors1, value1, error1, member_count)
    state = update(state, gains, anomaly, tile_weights(state, lon1, lat1, radius1))
    return state.astype(jnp.bfloat16)


def solution(mesh):
    placed = (P(None, None, "lat", "lon"), P(), P(), P(), P(), P(), P(), P())
    return jax.shard_map(
        shards, mesh=mesh, in_specs=placed, out_specs=P(None, None, "lat", "lon"), check_vma=False
    )
```

```python
import math

import jax
import jax.numpy as jnp
from jax import lax
from jax.sharding import PartitionSpec as P

STEPS = 2
BATCHES = 2
NB = 256


RATE = 0.4
DEPTHS = (1.0, 0.6, 0.35)
COUPLE = ((1.0, 0.5, 0.25), (0.5, 1.0, 0.5), (0.25, 0.5, 1.0))


def ring_pairs(size, step):
    return [(i, (i + step) % size) for i in range(size)]


def line_pairs(size, step):
    return [(i, i + step) for i in range(size) if 0 <= i + step < size]


def lon_edges(array):
    size = lax.axis_size("lon")
    up = [(i, (i + 1) % size) for i in range(size)]
    down = [((i + 1) % size, i) for i in range(size)]
    left = lax.ppermute(array[..., -1:], "lon", up)
    right = lax.ppermute(array[..., :1], "lon", down)
    return left, right


def lat_edges(array):
    size = lax.axis_size("lat")
    up = [(i, i + 1) for i in range(size - 1)]
    down = [(i + 1, i) for i in range(size - 1)]
    before = lax.ppermute(array[:, :, -1:, :], "lat", up)
    after = lax.ppermute(array[:, :, :1, :], "lat", down)
    return before, after


def zonal(values, left, right):
    following = jnp.concatenate([values[..., 1:], right], axis=3)
    preceding = jnp.concatenate([left, values[..., :-1]], axis=3)
    return 0.5 * (following - preceding)


def meridional(values, before, after):
    following = jnp.concatenate([values[:, :, 1:, :], after], axis=2)
    preceding = jnp.concatenate([before, values[:, :, :-1, :]], axis=2)
    return 0.5 * (following - preceding)


def couple(height):
    return jnp.stack(
        [
            COUPLE[k][0] * height[0] + COUPLE[k][1] * height[1] + COUPLE[k][2] * height[2]
            for k in range(3)
        ]
    )


def march_prediction(running_member_set, rotation_frequency):
    height = running_member_set[0:3]
    eastward_speed = running_member_set[3:6]
    merid_vel = running_member_set[6:9]
    depths = jnp.array(DEPTHS, jnp.float32)[:, None, None, None]
    v_before, v_after = lat_edges(merid_vel)
    height = height - RATE * depths * (
        zonal_inside(eastward_speed) + meridional(merid_vel, v_before, v_after)
    )
    pressure = couple(height)
    p_before, p_after = lat_edges(pressure)
    eastward_speed = (
        eastward_speed + RATE * rotation_frequency * merid_vel - RATE * zonal_inside(pressure)
    )
    merid_vel = (
        merid_vel
        - RATE * rotation_frequency * eastward_speed
        - RATE * meridional(pressure, p_before, p_after)
    )
    return jnp.concatenate([height, eastward_speed, merid_vel])


def zonal_inside(values):
    return zonal(values, values[..., :1], values[..., -1:])


def lon_widened(state, width):
    size = lax.axis_size("lon")
    order = (0, 3, 2, 1)
    left = lax.ppermute(jnp.transpose(state[..., -width:], order), "lon", ring_pairs(size, 1))
    right = lax.ppermute(jnp.transpose(state[..., :width], order), "lon", ring_pairs(size, -1))
    left = jnp.transpose(left, order)
    right = jnp.transpose(right, order)
    return jnp.concatenate([left, state, right], axis=3)


def statistics(priors, values, errors, member_count):
    mean_obs = jnp.mean(priors, axis=1, keepdims=True)
    anomaly = priors - mean_obs
    variance = jnp.sum(anomaly * anomaly, axis=1, keepdims=True) / (member_count - 1)
    obs_err = errors[:, None]
    denominator = variance + obs_err
    shrink = 1.0 / (1.0 + jnp.sqrt(obs_err / denominator))
    gains = (values[:, None] - mean_obs - shrink * anomaly) / denominator
    return (gains, anomaly)


def localize(cell_lon, cell_lat, lon_obs, lat_obs, radius_obs, grid_lon):
    lon_gap = (cell_lon[None, :] - lon_obs[:, None]) % grid_lon
    lon_gap = jnp.minimum(lon_gap, grid_lon - lon_gap)
    lat_gap = cell_lat[None, :] - lat_obs[:, None]
    distance_sq = (lon_gap * lon_gap + lat_gap * lat_gap).astype(jnp.float32)
    radius_sq = (radius_obs * radius_obs).astype(jnp.float32)[:, None]
    return jnp.square(jnp.maximum(1.0 - distance_sq / radius_sq, 0.0))


def neighbourhood_sum(table):
    lon_n = lax.axis_size("lon")
    lat_n = lax.axis_size("lat")
    row = (
        table
        + lax.ppermute(table, "lon", ring_pairs(lon_n, 1))
        + lax.ppermute(table, "lon", ring_pairs(lon_n, -1))
    )
    return (
        row
        + lax.ppermute(row, "lat", line_pairs(lat_n, 1))
        + lax.ppermute(row, "lat", line_pairs(lat_n, -1))
    )


def tile_origin(state):
    _, _, rows_tile, cols_tile = state.shape
    return lax.axis_index("lon") * cols_tile, lax.axis_index("lat") * rows_tile


REACH = BATCHES * (8 - 1)


def lat_shift(array, step):
    size = lax.axis_size("lat")
    pairs = [(i, i + step) for i in range(size) if 0 <= i + step < size]
    return lax.ppermute(array, "lat", pairs)


def band_table(wide, lon_obs, lat_obs, kind_obs, width):
    fields_count, _, rows_tile, wide_cols = wide.shape
    cols_tile = wide_cols - 2 * width
    grid_lon = cols_tile * lax.axis_size("lon")
    lon_base = lax.axis_index("lon") * cols_tile
    lat_base = lax.axis_index("lat") * rows_tile
    column = (lon_obs - lon_base + width) % grid_lon
    inside = (column >= width - REACH) & (column < width + cols_tile + REACH)
    row_hit = jnp.arange(rows_tile, dtype=jnp.int32)[None, :] == (lat_obs - lat_base)[:, None]
    col_hit = (jnp.arange(wide_cols, dtype=jnp.int32)[None, :] == column[:, None]) & inside[:, None]
    cell = (row_hit[:, :, None] & col_hit[:, None, :]).astype(jnp.float32)
    picked = jnp.einsum("jrc,fmrc->jfm", cell, wide, precision=lax.Precision.HIGHEST)
    field_hit = jnp.arange(fields_count, dtype=jnp.int32)[None, :] == kind_obs[:, None]
    return jnp.sum(jnp.where(field_hit[:, :, None], picked, 0.0), axis=1)


def owner_table(state, lon_obs, lat_obs, kind_obs):
    fields_count, _, rows_tile, cols_tile = state.shape
    lon_base, lat_base = tile_origin(state)
    row_hit = jnp.arange(rows_tile, dtype=jnp.int32)[None, :] == (lat_obs - lat_base)[:, None]
    col_hit = jnp.arange(cols_tile, dtype=jnp.int32)[None, :] == (lon_obs - lon_base)[:, None]
    cell = (row_hit[:, :, None] & col_hit[:, None, :]).astype(jnp.float32)
    picked = jnp.einsum("jrc,fmrc->jfm", cell, state, precision=lax.Precision.HIGHEST)
    field_hit = jnp.arange(fields_count, dtype=jnp.int32)[None, :] == kind_obs[:, None]
    return jnp.sum(jnp.where(field_hit[:, :, None], picked, 0.0), axis=1)


def update(state, gains, anomaly, weights):
    fields_count, member_count, rows_tile, cols_tile = state.shape
    flattened = state.reshape(fields_count, member_count, rows_tile * cols_tile)
    deviation = flattened - jnp.mean(flattened, axis=1, keepdims=True)
    covariance = jnp.einsum(
        "om,fmc->foc", anomaly, deviation, precision=lax.Precision.HIGH
    ) / (member_count - 1)
    increment = jnp.einsum(
        "om,foc->fmc", gains, covariance * weights[None], precision=lax.Precision.HIGH
    )
    return (flattened + increment).reshape(state.shape)


def tile_weights(state, lon_obs, lat_obs, radius_obs):
    _, _, rows_tile, cols_tile = state.shape
    lon_base, lat_base = tile_origin(state)
    grid_lon = cols_tile * lax.axis_size("lon")
    cell_lat = lat_base + jnp.repeat(jnp.arange(rows_tile, dtype=jnp.int32), cols_tile)
    cell_lon = lon_base + jnp.tile(jnp.arange(cols_tile, dtype=jnp.int32), rows_tile)
    return localize(cell_lon, cell_lat, lon_obs, lat_obs, radius_obs, grid_lon)


def shards(
    ensemble, obs_lon, obs_lat, observation_field, obs_radius, batch_order, obs_value, obs_error
):
    fields_count, member_count, rows_tile, cols_tile = ensemble.shape
    lat_index = lax.axis_index("lat")
    lat_count = lax.axis_size("lat")
    lon_size = lax.axis_size("lon")
    lat_size = lax.axis_size("lat")
    grid_lon = cols_tile * lon_size
    mesh_northing = rows_tile * lat_count
    row_global = (lat_index * rows_tile + jnp.arange(rows_tile, dtype=jnp.int32)).astype(
        jnp.float32
    )
    rotation_frequency = (2.0 * jnp.sin(math.pi * ((row_global + 0.5) / mesh_northing - 0.5)))[
        :, None
    ]
    ints = jnp.stack([obs_lon, obs_lat, observation_field, obs_radius])[:, batch_order]
    floats = jnp.stack([obs_value, obs_error])[:, batch_order]
    batches = [
        (ints[:, b * NB : (b + 1) * NB], floats[:, b * NB : (b + 1) * NB]) for b in range(BATCHES)
    ]
    width = 2 * STEPS + REACH
    state = lon_widened(ensemble, width)
    for step_index in range(STEPS):
        state = march_prediction(state, rotation_frequency)
    band = band_table(state, ints[0], ints[1], ints[2], width)
    state = state[..., width : width + cols_tile]

    (lon0, lat0, kind0, radius0), (value0, error0) = batches[0]
    (lon1, lat1, kind1, radius1), (value1, error1) = batches[1]
    table0 = band[:NB]
    both = band + lat_shift(band, 1) + lat_shift(band, -1)
    priors = both[:NB] + lat_shift(table0, 2) + lat_shift(table0, -2)
    raw1 = both[NB:]
    gains, anomaly = statistics(priors, value0, error0, member_count)
    deviation = raw1 - jnp.mean(raw1, axis=1, keepdims=True)
    covariance = jnp.einsum(
        "om,jm->oj", anomaly, deviation, precision=lax.Precision.HIGH
    ) / (member_count - 1)
    weights = localize(lon1, lat1, lon0, lat0, radius0, grid_lon)
    increment = jnp.einsum("om,oj->jm", gains, covariance * weights, precision=lax.Precision.HIGH)
    priors1 = raw1 + increment
    state = update(state, gains, anomaly, tile_weights(state, lon0, lat0, radius0))
    gains, anomaly = statistics(priors1, value1, error1, member_count)
    state = update(state, gains, anomaly, tile_weights(state, lon1, lat1, radius1))
    return state.astype(jnp.bfloat16)


def solution(mesh):
    placed = (P(None, None, "lat", "lon"), P(), P(), P(), P(), P(), P(), P())
    return jax.shard_map(
        shards, mesh=mesh, in_specs=placed, out_specs=P(None, None, "lat", "lon"), check_vma=False
    )
```

```python
import math

import jax
import jax.numpy as jnp
from jax import lax
from jax.sharding import PartitionSpec as P

STEPS = 2
BATCHES = 2
NB = 256


RATE = 0.4
DEPTHS = (1.0, 0.6, 0.35)
COUPLE = ((1.0, 0.5, 0.25), (0.5, 1.0, 0.5), (0.25, 0.5, 1.0))


def ring_pairs(size, step):
    return [(i, (i + step) % size) for i in range(size)]


def line_pairs(size, step):
    return [(i, i + step) for i in range(size) if 0 <= i + step < size]


def lon_edges(array):
    size = lax.axis_size("lon")
    up = [(i, (i + 1) % size) for i in range(size)]
    down = [((i + 1) % size, i) for i in range(size)]
    left = lax.ppermute(array[..., -1:], "lon", up)
    right = lax.ppermute(array[..., :1], "lon", down)
    return left, right


def lat_edges(array):
    size = lax.axis_size("lat")
    up = [(i, i + 1) for i in range(size - 1)]
    down = [(i + 1, i) for i in range(size - 1)]
    before = lax.ppermute(array[:, :, -1:, :], "lat", up)
    after = lax.ppermute(array[:, :, :1, :], "lat", down)
    return before, after


def zonal(values, left, right):
    following = jnp.concatenate([values[..., 1:], right], axis=3)
    preceding = jnp.concatenate([left, values[..., :-1]], axis=3)
    return 0.5 * (following - preceding)


def meridional(values, before, after):
    following = jnp.concatenate([values[:, :, 1:, :], after], axis=2)
    preceding = jnp.concatenate([before, values[:, :, :-1, :]], axis=2)
    return 0.5 * (following - preceding)


def couple(height):
    return jnp.stack(
        [
            COUPLE[k][0] * height[0] + COUPLE[k][1] * height[1] + COUPLE[k][2] * height[2]
            for k in range(3)
        ]
    )


def march_prediction(running_member_set, rotation_frequency):
    height = running_member_set[0:3]
    eastward_speed = running_member_set[3:6]
    merid_vel = running_member_set[6:9]
    depths = jnp.array(DEPTHS, jnp.float32)[:, None, None, None]
    v_before, v_after = lat_edges(merid_vel)
    height = height - RATE * depths * (
        zonal_inside(eastward_speed) + meridional(merid_vel, v_before, v_after)
    )
    pressure = couple(height)
    p_before, p_after = lat_edges(pressure)
    eastward_speed = (
        eastward_speed + RATE * rotation_frequency * merid_vel - RATE * zonal_inside(pressure)
    )
    merid_vel = (
        merid_vel
        - RATE * rotation_frequency * eastward_speed
        - RATE * meridional(pressure, p_before, p_after)
    )
    return jnp.concatenate([height, eastward_speed, merid_vel])


def zonal_inside(values):
    return zonal(values, values[..., :1], values[..., -1:])


def lon_widened(state, width):
    size = lax.axis_size("lon")
    order = (0, 3, 2, 1)
    left = lax.ppermute(jnp.transpose(state[..., -width:], order), "lon", ring_pairs(size, 1))
    right = lax.ppermute(jnp.transpose(state[..., :width], order), "lon", ring_pairs(size, -1))
    left = jnp.transpose(left, order)
    right = jnp.transpose(right, order)
    return jnp.concatenate([left, state, right], axis=3)


def statistics(priors, values, errors, member_count):
    mean_obs = jnp.mean(priors, axis=1, keepdims=True)
    anomaly = priors - mean_obs
    variance = jnp.sum(anomaly * anomaly, axis=1, keepdims=True) / (member_count - 1)
    obs_err = errors[:, None]
    denominator = variance + obs_err
    shrink = 1.0 / (1.0 + jnp.sqrt(obs_err / denominator))
    gains = (values[:, None] - mean_obs - shrink * anomaly) / denominator
    return (gains, anomaly)


def localize(cell_lon, cell_lat, lon_obs, lat_obs, radius_obs, grid_lon):
    lon_gap = (cell_lon[None, :] - lon_obs[:, None]) % grid_lon
    lon_gap = jnp.minimum(lon_gap, grid_lon - lon_gap)
    lat_gap = cell_lat[None, :] - lat_obs[:, None]
    distance_sq = (lon_gap * lon_gap + lat_gap * lat_gap).astype(jnp.float32)
    radius_sq = (radius_obs * radius_obs).astype(jnp.float32)[:, None]
    return jnp.square(jnp.maximum(1.0 - distance_sq / radius_sq, 0.0))


def neighbourhood_sum(table):
    lon_n = lax.axis_size("lon")
    lat_n = lax.axis_size("lat")
    row = (
        table
        + lax.ppermute(table, "lon", ring_pairs(lon_n, 1))
        + lax.ppermute(table, "lon", ring_pairs(lon_n, -1))
    )
    return (
        row
        + lax.ppermute(row, "lat", line_pairs(lat_n, 1))
        + lax.ppermute(row, "lat", line_pairs(lat_n, -1))
    )


def tile_origin(state):
    _, _, rows_tile, cols_tile = state.shape
    return lax.axis_index("lon") * cols_tile, lax.axis_index("lat") * rows_tile


REACH = BATCHES * (8 - 1)


def lat_shift(array, step):
    size = lax.axis_size("lat")
    pairs = [(i, i + step) for i in range(size) if 0 <= i + step < size]
    return lax.ppermute(array, "lat", pairs)


def band_table(wide, lon_obs, lat_obs, kind_obs, width):
    fields_count, _, rows_tile, wide_cols = wide.shape
    cols_tile = wide_cols - 2 * width
    grid_lon = cols_tile * lax.axis_size("lon")
    lon_base = lax.axis_index("lon") * cols_tile
    lat_base = lax.axis_index("lat") * rows_tile
    column = (lon_obs - lon_base + width) % grid_lon
    inside = (column >= width - REACH) & (column < width + cols_tile + REACH)
    row_hit = jnp.arange(rows_tile, dtype=jnp.int32)[None, :] == (lat_obs - lat_base)[:, None]
    col_hit = (jnp.arange(wide_cols, dtype=jnp.int32)[None, :] == column[:, None]) & inside[:, None]
    cell = (row_hit[:, :, None] & col_hit[:, None, :]).astype(jnp.float32)
    picked = jnp.einsum("jrc,fmrc->jfm", cell, wide, precision=lax.Precision.HIGHEST)
    field_hit = jnp.arange(fields_count, dtype=jnp.int32)[None, :] == kind_obs[:, None]
    return jnp.sum(jnp.where(field_hit[:, :, None], picked, 0.0), axis=1)


def owner_table(state, lon_obs, lat_obs, kind_obs):
    fields_count, _, rows_tile, cols_tile = state.shape
    lon_base, lat_base = tile_origin(state)
    row_hit = jnp.arange(rows_tile, dtype=jnp.int32)[None, :] == (lat_obs - lat_base)[:, None]
    col_hit = jnp.arange(cols_tile, dtype=jnp.int32)[None, :] == (lon_obs - lon_base)[:, None]
    cell = (row_hit[:, :, None] & col_hit[:, None, :]).astype(jnp.float32)
    picked = jnp.einsum("jrc,fmrc->jfm", cell, state, precision=lax.Precision.HIGHEST)
    field_hit = jnp.arange(fields_count, dtype=jnp.int32)[None, :] == kind_obs[:, None]
    return jnp.sum(jnp.where(field_hit[:, :, None], picked, 0.0), axis=1)


def update(state, gains, anomaly, weights):
    fields_count, member_count, rows_tile, cols_tile = state.shape
    flattened = state.reshape(fields_count, member_count, rows_tile * cols_tile)
    deviation = flattened - jnp.mean(flattened, axis=1, keepdims=True)
    covariance = jnp.einsum(
        "om,fmc->foc", anomaly, deviation, precision=lax.Precision.HIGH
    ) / (member_count - 1)
    increment = jnp.einsum(
        "om,foc->fmc", gains, covariance * weights[None], precision=lax.Precision.HIGH
    )
    return (flattened + increment).reshape(state.shape)


def tile_weights(state, lon_obs, lat_obs, radius_obs):
    _, _, rows_tile, cols_tile = state.shape
    lon_base, lat_base = tile_origin(state)
    grid_lon = cols_tile * lax.axis_size("lon")
    cell_lat = lat_base + jnp.repeat(jnp.arange(rows_tile, dtype=jnp.int32), cols_tile)
    cell_lon = lon_base + jnp.tile(jnp.arange(cols_tile, dtype=jnp.int32), rows_tile)
    return localize(cell_lon, cell_lat, lon_obs, lat_obs, radius_obs, grid_lon)


def shards(
    ensemble, obs_lon, obs_lat, observation_field, obs_radius, batch_order, obs_value, obs_error
):
    fields_count, member_count, rows_tile, cols_tile = ensemble.shape
    lat_index = lax.axis_index("lat")
    lat_count = lax.axis_size("lat")
    lon_size = lax.axis_size("lon")
    lat_size = lax.axis_size("lat")
    grid_lon = cols_tile * lon_size
    mesh_northing = rows_tile * lat_count
    row_global = (lat_index * rows_tile + jnp.arange(rows_tile, dtype=jnp.int32)).astype(
        jnp.float32
    )
    rotation_frequency = (2.0 * jnp.sin(math.pi * ((row_global + 0.5) / mesh_northing - 0.5)))[
        :, None
    ]
    ints = jnp.stack([obs_lon, obs_lat, observation_field, obs_radius])[:, batch_order]
    floats = jnp.stack([obs_value, obs_error])[:, batch_order]
    batches = [
        (ints[:, b * NB : (b + 1) * NB], floats[:, b * NB : (b + 1) * NB]) for b in range(BATCHES)
    ]
    width = 2 * STEPS + REACH
    state = lon_widened(ensemble, width)
    for step_index in range(STEPS):
        state = march_prediction(state, rotation_frequency)
    band = band_table(state, ints[0], ints[1], ints[2], width)
    state = state[..., width : width + cols_tile]

    (lon0, lat0, kind0, radius0), (value0, error0) = batches[0]
    (lon1, lat1, kind1, radius1), (value1, error1) = batches[1]
    table0 = band[:NB]
    both = band + lat_shift(band, 1) + lat_shift(band, -1)
    raw1 = both[NB:]
    gains, anomaly = statistics(both[:NB], value0, error0, member_count)
    state = update(state, gains, anomaly, tile_weights(state, lon0, lat0, radius0))
    table0, state = lax.optimization_barrier((table0, state))
    priors = both[:NB] + lat_shift(table0, 2) + lat_shift(table0, -2)
    gains, anomaly = statistics(priors, value0, error0, member_count)
    deviation = raw1 - jnp.mean(raw1, axis=1, keepdims=True)
    covariance = jnp.einsum(
        "om,jm->oj", anomaly, deviation, precision=lax.Precision.HIGH
    ) / (member_count - 1)
    weights = localize(lon1, lat1, lon0, lat0, radius0, grid_lon)
    increment = jnp.einsum("om,oj->jm", gains, covariance * weights, precision=lax.Precision.HIGH)
    priors1 = raw1 + increment
    gains, anomaly = statistics(priors1, value1, error1, member_count)
    state = update(state, gains, anomaly, tile_weights(state, lon1, lat1, radius1))
    return state.astype(jnp.bfloat16)


def solution(mesh):
    placed = (P(None, None, "lat", "lon"), P(), P(), P(), P(), P(), P(), P())
    return jax.shard_map(
        shards, mesh=mesh, in_specs=placed, out_specs=P(None, None, "lat", "lon"), check_vma=False
    )
```

```python
import math

import jax
import jax.numpy as jnp
from jax import lax
from jax.sharding import PartitionSpec as P

STEPS = 2
BATCHES = 2
NB = 256


RATE = 0.4
DEPTHS = (1.0, 0.6, 0.35)
COUPLE = ((1.0, 0.5, 0.25), (0.5, 1.0, 0.5), (0.25, 0.5, 1.0))


def ring_pairs(size, step):
    return [(i, (i + step) % size) for i in range(size)]


def line_pairs(size, step):
    return [(i, i + step) for i in range(size) if 0 <= i + step < size]


def lon_edges(array):
    size = lax.axis_size("lon")
    up = [(i, (i + 1) % size) for i in range(size)]
    down = [((i + 1) % size, i) for i in range(size)]
    left = lax.ppermute(array[..., -1:], "lon", up)
    right = lax.ppermute(array[..., :1], "lon", down)
    return left, right


def lat_edges(array):
    size = lax.axis_size("lat")
    up = [(i, i + 1) for i in range(size - 1)]
    down = [(i + 1, i) for i in range(size - 1)]
    before = lax.ppermute(array[:, :, -1:, :], "lat", up)
    after = lax.ppermute(array[:, :, :1, :], "lat", down)
    return before, after


def zonal(values, left, right):
    following = jnp.concatenate([values[..., 1:], right], axis=3)
    preceding = jnp.concatenate([left, values[..., :-1]], axis=3)
    return 0.5 * (following - preceding)


def meridional(values, before, after):
    following = jnp.concatenate([values[:, :, 1:, :], after], axis=2)
    preceding = jnp.concatenate([before, values[:, :, :-1, :]], axis=2)
    return 0.5 * (following - preceding)


def couple(height):
    return jnp.stack(
        [
            COUPLE[k][0] * height[0] + COUPLE[k][1] * height[1] + COUPLE[k][2] * height[2]
            for k in range(3)
        ]
    )


def march_prediction(running_member_set, rotation_frequency):
    height = running_member_set[0:3]
    eastward_speed = running_member_set[3:6]
    merid_vel = running_member_set[6:9]
    depths = jnp.array(DEPTHS, jnp.float32)[:, None, None, None]
    v_before, v_after = lat_edges(merid_vel)
    height = height - RATE * depths * (
        zonal_inside(eastward_speed) + meridional(merid_vel, v_before, v_after)
    )
    pressure = couple(height)
    p_before, p_after = lat_edges(pressure)
    eastward_speed = (
        eastward_speed + RATE * rotation_frequency * merid_vel - RATE * zonal_inside(pressure)
    )
    merid_vel = (
        merid_vel
        - RATE * rotation_frequency * eastward_speed
        - RATE * meridional(pressure, p_before, p_after)
    )
    return jnp.concatenate([height, eastward_speed, merid_vel])


def zonal_inside(values):
    return zonal(values, values[..., :1], values[..., -1:])


def lon_widened(state, width):
    size = lax.axis_size("lon")
    order = (0, 3, 2, 1)
    left = lax.ppermute(jnp.transpose(state[..., -width:], order), "lon", ring_pairs(size, 1))
    right = lax.ppermute(jnp.transpose(state[..., :width], order), "lon", ring_pairs(size, -1))
    left = jnp.transpose(left, order)
    right = jnp.transpose(right, order)
    return jnp.concatenate([left, state, right], axis=3)


def statistics(priors, values, errors, member_count):
    mean_obs = jnp.mean(priors, axis=1, keepdims=True)
    anomaly = priors - mean_obs
    variance = jnp.sum(anomaly * anomaly, axis=1, keepdims=True) / (member_count - 1)
    obs_err = errors[:, None]
    denominator = variance + obs_err
    shrink = 1.0 / (1.0 + jnp.sqrt(obs_err / denominator))
    gains = (values[:, None] - mean_obs - shrink * anomaly) / denominator
    return (gains, anomaly)


def localize(cell_lon, cell_lat, lon_obs, lat_obs, radius_obs, grid_lon):
    lon_gap = (cell_lon[None, :] - lon_obs[:, None]) % grid_lon
    lon_gap = jnp.minimum(lon_gap, grid_lon - lon_gap)
    lat_gap = cell_lat[None, :] - lat_obs[:, None]
    distance_sq = (lon_gap * lon_gap + lat_gap * lat_gap).astype(jnp.float32)
    radius_sq = (radius_obs * radius_obs).astype(jnp.float32)[:, None]
    return jnp.square(jnp.maximum(1.0 - distance_sq / radius_sq, 0.0))


def neighbourhood_sum(table):
    lon_n = lax.axis_size("lon")
    lat_n = lax.axis_size("lat")
    row = (
        table
        + lax.ppermute(table, "lon", ring_pairs(lon_n, 1))
        + lax.ppermute(table, "lon", ring_pairs(lon_n, -1))
    )
    return (
        row
        + lax.ppermute(row, "lat", line_pairs(lat_n, 1))
        + lax.ppermute(row, "lat", line_pairs(lat_n, -1))
    )


def tile_origin(state):
    _, _, rows_tile, cols_tile = state.shape
    return lax.axis_index("lon") * cols_tile, lax.axis_index("lat") * rows_tile


REACH = BATCHES * (8 - 1)


def lat_shift(array, step):
    size = lax.axis_size("lat")
    pairs = [(i, i + step) for i in range(size) if 0 <= i + step < size]
    return lax.ppermute(array, "lat", pairs)


def band_table(wide, lon_obs, lat_obs, kind_obs, width):
    fields_count, _, rows_tile, wide_cols = wide.shape
    cols_tile = wide_cols - 2 * width
    grid_lon = cols_tile * lax.axis_size("lon")
    lon_base = lax.axis_index("lon") * cols_tile
    lat_base = lax.axis_index("lat") * rows_tile
    column = (lon_obs - lon_base + width) % grid_lon
    inside = (column >= width - REACH) & (column < width + cols_tile + REACH)
    row_hit = jnp.arange(rows_tile, dtype=jnp.int32)[None, :] == (lat_obs - lat_base)[:, None]
    col_hit = (jnp.arange(wide_cols, dtype=jnp.int32)[None, :] == column[:, None]) & inside[:, None]
    cell = (row_hit[:, :, None] & col_hit[:, None, :]).astype(jnp.float32)
    picked = jnp.einsum("jrc,fmrc->jfm", cell, wide, precision=lax.Precision.HIGH)
    field_hit = jnp.arange(fields_count, dtype=jnp.int32)[None, :] == kind_obs[:, None]
    return jnp.sum(jnp.where(field_hit[:, :, None], picked, 0.0), axis=1)


def owner_table(state, lon_obs, lat_obs, kind_obs):
    fields_count, _, rows_tile, cols_tile = state.shape
    lon_base, lat_base = tile_origin(state)
    row_hit = jnp.arange(rows_tile, dtype=jnp.int32)[None, :] == (lat_obs - lat_base)[:, None]
    col_hit = jnp.arange(cols_tile, dtype=jnp.int32)[None, :] == (lon_obs - lon_base)[:, None]
    cell = (row_hit[:, :, None] & col_hit[:, None, :]).astype(jnp.float32)
    picked = jnp.einsum("jrc,fmrc->jfm", cell, state, precision=lax.Precision.HIGHEST)
    field_hit = jnp.arange(fields_count, dtype=jnp.int32)[None, :] == kind_obs[:, None]
    return jnp.sum(jnp.where(field_hit[:, :, None], picked, 0.0), axis=1)


def update(state, gains, anomaly, weights):
    fields_count, member_count, rows_tile, cols_tile = state.shape
    flattened = state.reshape(fields_count, member_count, rows_tile * cols_tile)
    deviation = flattened - jnp.mean(flattened, axis=1, keepdims=True)
    covariance = jnp.einsum(
        "om,fmc->foc", anomaly, deviation, precision=lax.Precision.HIGH
    ) / (member_count - 1)
    increment = jnp.einsum(
        "om,foc->fmc", gains, covariance * weights[None], precision=lax.Precision.HIGH
    )
    return (flattened + increment).reshape(state.shape)


def tile_weights(state, lon_obs, lat_obs, radius_obs):
    _, _, rows_tile, cols_tile = state.shape
    lon_base, lat_base = tile_origin(state)
    grid_lon = cols_tile * lax.axis_size("lon")
    cell_lat = lat_base + jnp.repeat(jnp.arange(rows_tile, dtype=jnp.int32), cols_tile)
    cell_lon = lon_base + jnp.tile(jnp.arange(cols_tile, dtype=jnp.int32), rows_tile)
    return localize(cell_lon, cell_lat, lon_obs, lat_obs, radius_obs, grid_lon)


def shards(
    ensemble, obs_lon, obs_lat, observation_field, obs_radius, batch_order, obs_value, obs_error
):
    fields_count, member_count, rows_tile, cols_tile = ensemble.shape
    lat_index = lax.axis_index("lat")
    lat_count = lax.axis_size("lat")
    lon_size = lax.axis_size("lon")
    lat_size = lax.axis_size("lat")
    grid_lon = cols_tile * lon_size
    mesh_northing = rows_tile * lat_count
    row_global = (lat_index * rows_tile + jnp.arange(rows_tile, dtype=jnp.int32)).astype(
        jnp.float32
    )
    rotation_frequency = (2.0 * jnp.sin(math.pi * ((row_global + 0.5) / mesh_northing - 0.5)))[
        :, None
    ]
    ints = jnp.stack([obs_lon, obs_lat, observation_field, obs_radius])[:, batch_order]
    floats = jnp.stack([obs_value, obs_error])[:, batch_order]
    batches = [
        (ints[:, b * NB : (b + 1) * NB], floats[:, b * NB : (b + 1) * NB]) for b in range(BATCHES)
    ]
    width = 2 * STEPS + REACH
    state = lon_widened(ensemble, width)
    for step_index in range(STEPS):
        state = march_prediction(state, rotation_frequency)
    band = band_table(state, ints[0], ints[1], ints[2], width)
    state = state[..., width : width + cols_tile]

    (lon0, lat0, kind0, radius0), (value0, error0) = batches[0]
    (lon1, lat1, kind1, radius1), (value1, error1) = batches[1]
    table0 = band[:NB]
    both = band + lat_shift(band, 1) + lat_shift(band, -1)
    priors = both[:NB] + lat_shift(table0, 2) + lat_shift(table0, -2)
    raw1 = both[NB:]
    gains, anomaly = statistics(priors, value0, error0, member_count)
    deviation = raw1 - jnp.mean(raw1, axis=1, keepdims=True)
    covariance = jnp.einsum(
        "om,jm->oj", anomaly, deviation, precision=lax.Precision.HIGH
    ) / (member_count - 1)
    weights = localize(lon1, lat1, lon0, lat0, radius0, grid_lon)
    increment = jnp.einsum("om,oj->jm", gains, covariance * weights, precision=lax.Precision.HIGH)
    priors1 = raw1 + increment
    state = update(state, gains, anomaly, tile_weights(state, lon0, lat0, radius0))
    gains, anomaly = statistics(priors1, value1, error1, member_count)
    state = update(state, gains, anomaly, tile_weights(state, lon1, lat1, radius1))
    return state.astype(jnp.bfloat16)


def solution(mesh):
    placed = (P(None, None, "lat", "lon"), P(), P(), P(), P(), P(), P(), P())
    return jax.shard_map(
        shards, mesh=mesh, in_specs=placed, out_specs=P(None, None, "lat", "lon"), check_vma=False
    )
```
